1024 devices in a mesh: span: 32 (over z_lo, core), wall: 32 (over z_hi, y, x).
Axes of the slice: x: 4, y: 4, z: 32 (z_hi: 2, z_lo: 16; z = z_hi * 16 + z_lo), core: 2. Of those that a mesh axis runs over, the one named last changes fastest.
Arguments:
- field: float32 [5, 5, 5, 32, 64, 128], P(None, None, None, 'span', 'wall'), may hold values from -6 to 6
- velocity: float32 [3, 5, 5, 5, 32, 64, 128], P(None, None, None, None, 'span', 'wall'), may hold values from -6 to 6
- cells: int32 [131072], P(('span', 'wall')), may hold values from 0 to 255
- destination: int32 [131072, 1], P(('span', 'wall')), may hold values from 0 to 31; in each aligned block of 128 rows (0 to 127, 128 to 255, ...) at most 16 rows name the same one
- targets: bfloat16 [131072, 128], P(('span', 'wall')), may hold values from -6 to 6
- weight_in: bfloat16 [32, 128, 256], P('span'), may hold values from -0.5 to 0.5
- weight_two: bfloat16 [32, 256, 256], P('span'), may hold values from -0.375 to 0.375
- weight_three: bfloat16 [32, 256, 256], P('span'), may hold values from -0.375 to 0.375
- weight_four: bfloat16 [32, 256, 256], P('span'), may hold values from -0.375 to 0.375
- weight_out: bfloat16 [32, 256, 128], P('span'), may hold values from -0.375 to 0.375
Outputs:
- new_field: float32 [5, 5, 5, 32, 64, 128], P(None, None, None, 'span', 'wall')
- grad_in: float32 [32, 128, 256], P('span')
- grad_two: float32 [32, 256, 256], P('span')
- grad_three: float32 [32, 256, 256], P('span')
- grad_four: float32 [32, 256, 256], P('span')
- grad_out: float32 [32, 256, 128], P('span')
The draws below stay inside these ranges and needn't reach their ends.
Inputs may be any that keep to these rules, and one draw needn't show every extreme that they name: `cells`: A local element index of the owning device. `destination`: among the 128 rows of one device at most 16 name the same station, and in every draw some device has exactly 16 rows naming one station.
All inputs are finite; a program needn't handle non-finite values.
Results may differ from the reference program's by a relative error of at most 0.0065.
Values may be sent and summed in bfloat16 or wider, within the bound.
No kernel may reach another device: no remote copies, remote signals or barrier semaphores. Data moves between devices by JAX's collectives and lax.ppermute only.
A program may use at most 32 MiB of HBM per device.

```python
import math
import jax
import jax.numpy as jnp
import numpy as np
from jax import lax

P_SIZE = 5
EA = 1
EB = 2
EC = 128
S = 128
HID = 256
OUT = 128
CAP = 16
FEAT = 128
NA = 32
NB = 64
ROWS = 131072
N_SPAN = 32
N_WALL = 32


def set_ends(entries, own_key, least, top_value):
    spot = [jax.random.randint(jax.random.fold_in(own_key, axis), (), 0, length) for axis, length in enumerate(entries.shape)]
    widest = entries.shape.index(max(entries.shape))
    neighbour = spot[:widest] + [(spot[widest] + 1) % entries.shape[widest]] + spot[widest + 1:]
    return entries.at[tuple(spot)].set(least).at[tuple(neighbour)].set(top_value)


def levels(own_key, extent, cuts, least, high):
    gain = 1.0
    for axis_at, parts in cuts:
        steps = jax.random.uniform(jax.random.fold_in(jax.random.fold_in(own_key, 6), axis_at), (parts,), jnp.float32, least / len(cuts), high / len(cuts))
        gain = gain * jnp.repeat(jnp.exp(steps), extent[axis_at] // parts).reshape((-1,) + (1,) * (len(extent) - 1 - axis_at))
    return gain


def assign_block(key, own, number, rows, count, top, reach, lean):
    ranking = jax.random.permutation(key, count)
    packed, common = load_shares(count, rows * top, reach, lean, True), load_shares(count, rows * top, reach, lean, False)
    places = jnp.arange(count)

    def named(sizes, turn):
        used = int((sizes > 0).sum())
        fixed = max(1, used // 4)
        passed = fixed + (places - fixed + turn * (used - fixed)) % max(1, count - fixed)
        return jnp.zeros((count,), jnp.int32).at[ranking[jnp.where(places < fixed, places, passed)]].set(jnp.asarray(sizes, jnp.int32))

    sizes = jnp.where(number % 4 == 0, named(packed, number // 4), named(common, number - number // 4 - 1))
    mixed = jax.random.permutation(jax.random.fold_in(own, 3), count)
    giver, taker = mixed[0:count // 2 * 2:2], mixed[1:count // 2 * 2:2]
    margin = jnp.minimum(sizes[giver] - 1, reach - sizes[taker]) // 2
    margin = jnp.where((giver == ranking[0]) | (taker == ranking[0]) | (sizes[taker] == 0), 0, jnp.maximum(margin, 0))
    passed = jax.random.randint(jax.random.fold_in(own, 4), (count // 2,), 0, 1 << 20) % (margin + 1)
    sizes = sizes.at[giver].add(-passed).at[taker].add(passed)
    members = jnp.searchsorted(jnp.cumsum(sizes), jnp.arange(rows * top), side="right").astype(jnp.int32)
    grid = members.reshape(top, rows).T
    grid = grid[jax.random.permutation(jax.random.fold_in(own, 1), rows)]
    turn = jax.random.randint(jax.random.fold_in(own, 2), (rows, 1), 0, top)
    return jnp.take_along_axis(grid, (jnp.arange(top)[None, :] + turn) % top, axis=1)


def load_shares(number_of, total, reach, skew, full):
    portions = [(1 << 20) // math.isqrt(grade ** skew) + 1 for grade in range(1, number_of + 1)]
    largest = reach if full else min(reach, max(-(-total // number_of), total * portions[0] // sum(portions)))
    least = 1 if total - largest >= number_of - 1 else 0
    holding, spare = [largest] + [least] * (number_of - 1), total - largest - least * (number_of - 1)
    while spare > 0:
        free = [i for i in range(1, number_of) if holding[i] < largest] or [i for i in range(1, number_of) if holding[i] < reach]
        whole, left = sum([portions[i] for i in free]), spare
        for i in free:
            extra = min(reach - holding[i], max(1, left * portions[i] // whole), spare)
            holding[i] = holding[i] + extra
            spare = spare - extra
    return np.array(holding)


def centred(own_key, shape, scale, reach, shards=(), kind=jnp.bfloat16):
    level = levels(own_key, shape, shards, -0.22, 0.18) if shards else 1.0
    result = jax.random.normal(own_key, shape, jnp.float32) * scale * level
    return jnp.minimum(jnp.maximum(result, -reach), reach).astype(kind)


def setup_inputs(seed: int = 0) -> dict:
    key_list = jax.random.split(jax.random.key(seed), 11)
    field = centred(key_list[0], (P_SIZE, P_SIZE, P_SIZE, NA, NB, EC), 1.0, 6.0, ((3, 32), (4, 32)), jnp.float32)
    velocity = centred(key_list[1], (3, P_SIZE, P_SIZE, P_SIZE, NA, NB, EC), 1.0, 6.0, ((4, 32), (5, 32)), jnp.float32)
    cells = set_ends(jax.random.randint(key_list[2], (ROWS,), 0, EA * EB * EC), jax.random.fold_in(key_list[2], 1), 0, (EA * EB * EC) - 1).astype(jnp.int32)
    destination_keys = jax.random.split(jax.random.fold_in(key_list[3], 1), ROWS // S)
    destination_turns = jax.random.permutation(jax.random.fold_in(key_list[3], 3), ROWS // S)
    destination = jax.vmap(lambda own, number: assign_block(jax.random.fold_in(key_list[3], 2), own, number, S, N_SPAN, 1, CAP, 2))(destination_keys, destination_turns).reshape((ROWS, 1))
    targets = centred(key_list[4], (ROWS, OUT), 1.0, 6.0, ((0, 1024),))
    weight_in = centred(key_list[5], (N_SPAN, FEAT, HID), FEAT ** -0.5, 0.5, ((0, 32),))
    weight_two = centred(key_list[6], (N_SPAN, HID, HID), HID ** -0.5, 0.375, ((0, 32),))
    weight_three = centred(key_list[7], (N_SPAN, HID, HID), HID ** -0.5, 0.375, ((0, 32),))
    weight_four = centred(key_list[8], (N_SPAN, HID, HID), HID ** -0.5, 0.375, ((0, 32),))
    weight_out = centred(key_list[9], (N_SPAN, HID, OUT), HID ** -0.5, 0.375, ((0, 32),))
    return dict(field=field, velocity=velocity, cells=cells, destination=destination, targets=targets, weight_in=weight_in, weight_two=weight_two, weight_three=weight_three, weight_four=weight_four, weight_out=weight_out)


step_scale = 0.04

def legendre_pair(order, point):
    value_prev = 1.0
    value_now = point
    slope_prev = 0.0
    slope_now = 1.0
    if order == 0:
        return (1.0, 0.0)
    for degree in range(1, order):
        value_next = ((2 * degree + 1) * point * value_now - degree * value_prev) / (degree + 1)
        slope_next = slope_prev + (2 * degree + 1) * value_now
        value_prev, value_now = (value_now, value_next)
        slope_prev, slope_now = (slope_now, slope_next)
    return (value_now, slope_now)

def gauss_nodes(count):
    found = []
    for index in range(count):
        guess = math.cos(math.pi * (index + 0.75) / (count + 0.5))
        for sweep in range(60):
            value, slope = legendre_pair(count, guess)
            guess = guess - value / slope
        found.append(guess)
    return sorted(found)

def fr_tables():
    nodes = gauss_nodes(P_SIZE)
    bary = []
    for j in range(P_SIZE):
        product = 1.0
        for m in range(P_SIZE):
            if m != j:
                product = product * (nodes[j] - nodes[m])
        bary.append(1.0 / product)
    deriv = [[0.0] * P_SIZE for row_index in range(P_SIZE)]
    for i in range(P_SIZE):
        for j in range(P_SIZE):
            if i != j:
                deriv[i][j] = bary[j] / bary[i] / (nodes[i] - nodes[j])
        deriv[i][i] = -sum((deriv[i][j] for j in range(P_SIZE) if j != i))

    def basis_at(point):
        values = []
        for j in range(P_SIZE):
            product = 1.0
            for m in range(P_SIZE):
                if m != j:
                    product = product * (point - nodes[m]) / (nodes[j] - nodes[m])
            values.append(product)
        return values
    left_value = basis_at(-1.0)
    right_value = basis_at(1.0)
    sign = (-1.0) ** P_SIZE
    slope_left = [0.5 * sign * (legendre_pair(P_SIZE, x)[1] - legendre_pair(P_SIZE - 1, x)[1]) for x in nodes]
    slope_right = [-slope_left[P_SIZE - 1 - i] for i in range(P_SIZE)]
    return tuple((jnp.asarray(table, jnp.float32) for table in (deriv, left_value, right_value, slope_left, slope_right)))

def along(matrix, field, axis):
    return jnp.moveaxis(jnp.tensordot(matrix, field, axes=([1], [axis]), precision=lax.Precision.HIGHEST), 0, axis)

def at_face(vector, field, axis):
    return jnp.tensordot(vector, field, axes=([0], [axis]), precision=lax.Precision.HIGHEST)

def spread(face, vector, axis, ndim):
    target_shape = [1] * ndim
    target_shape[axis] = vector.shape[0]
    return jnp.expand_dims(face, axis) * vector.reshape(target_shape)

def upwind(state_before, speed_before, state_after, speed_after):
    mean_speed = 0.5 * (speed_before + speed_after)
    return 0.5 * mean_speed * (state_before + state_after) - 0.5 * jnp.abs(mean_speed) * (state_after - state_before)

def face_states(field, speed, axis, tables):
    left_value = tables[1]
    right_value = tables[2]
    return (at_face(left_value, field, axis), at_face(left_value, speed, axis), at_face(right_value, field, axis), at_face(right_value, speed, axis))

def divergence(field, speed, axis, own, before, after, tables):
    deriv, left_value, right_value, slope_left, slope_right = tables
    flux = speed * field
    volume = along(deriv, flux, axis)
    flux_left = at_face(left_value, flux, axis)
    flux_right = at_face(right_value, flux, axis)
    common_left = upwind(before[0], before[1], own[0], own[1])
    common_right = upwind(own[2], own[3], after[0], after[1])
    return volume + spread(common_left - flux_left, slope_left, axis, field.ndim) + spread(common_right - flux_right, slope_right, axis, field.ndim)

def forward(inputs, weights):
    acts = [inputs]
    pres = []
    hidden = inputs
    for layer in weights[:-1]:
        pre = jnp.dot(hidden, layer, preferred_element_type=jnp.float32)
        pres.append(pre)
        hidden = jax.nn.silu(pre).astype(jnp.bfloat16)
        acts.append(hidden)
    return (jnp.dot(hidden, weights[-1], preferred_element_type=jnp.float32), acts, pres)

def backward_layer(error, weight, pre):
    back = lax.dot_general(error, weight, (((1,), (1,)), ((), ())), preferred_element_type=jnp.float32)
    sigma = jax.nn.sigmoid(pre)
    return (back * sigma * (1.0 + pre * (1.0 - sigma))).astype(jnp.bfloat16)

def weight_grad(act, error):
    return lax.dot_general(act, error, (((0,), (0,)), ((), ())), preferred_element_type=jnp.float32)

def row_grads(inputs, targets, row_scale, weights):
    output, acts, pres = forward(inputs, weights)
    error = (row_scale[:, None] * (output - targets.astype(jnp.float32))).astype(jnp.bfloat16)
    grads = [None] * 5
    grads[4] = weight_grad(acts[4], error)
    for layer_index in range(3, -1, -1):
        error = backward_layer(error, weights[layer_index + 1], pres[layer_index])
        grads[layer_index] = weight_grad(acts[layer_index], error)
    return tuple(grads)

def shift_down(face, axis):
    widths = [(1, 0) if dim_index == axis else (0, 0) for dim_index in range(face.ndim)]
    return lax.slice_in_dim(jnp.pad(face, widths), 0, face.shape[axis], axis=axis)

def shift_up(face, axis):
    widths = [(0, 1) if dim_index == axis else (0, 0) for dim_index in range(face.ndim)]
    return lax.slice_in_dim(jnp.pad(face, widths), 1, face.shape[axis] + 1, axis=axis)

def reference(field, velocity, cells, destination, targets, weight_in, weight_two, weight_three, weight_four, weight_out):
    tables = fr_tables()
    total = jnp.zeros_like(field)
    for direction in range(3):
        speed = velocity[direction]
        own = face_states(field, speed, direction, tables)
        face_axis = 2 + direction
        if direction < 2:
            before = (shift_down(own[2], face_axis), shift_down(own[3], face_axis))
            after = (shift_up(own[0], face_axis), shift_up(own[1], face_axis))
        else:
            before = (jnp.roll(own[2], 1, face_axis), jnp.roll(own[3], 1, face_axis))
            after = (jnp.roll(own[0], -1, face_axis), jnp.roll(own[1], -1, face_axis))
        total = total + divergence(field, speed, direction, own, before, after, tables)
    new_field = field - step_scale * total
    devices_all = N_SPAN * N_WALL
    local_count = EA * EB * EC
    point_values = new_field.reshape(P_SIZE * P_SIZE * P_SIZE, N_SPAN, EA, N_WALL, EB, EC)
    point_values = point_values.transpose(1, 3, 0, 2, 4, 5).reshape(devices_all, P_SIZE * P_SIZE * P_SIZE, local_count)
    speed_means = lax.optimization_barrier(jnp.mean(velocity.reshape(3, P_SIZE * P_SIZE * P_SIZE, N_SPAN, EA, N_WALL, EB, EC), axis=1))
    speed_means = speed_means.transpose(1, 3, 0, 2, 4, 5).reshape(devices_all, 3, local_count)
    values = jnp.concatenate([point_values, speed_means], axis=1)
    picked = jnp.take_along_axis(values, cells.reshape(devices_all, 1, S).astype(jnp.int32), axis=2)
    rows = picked.transpose(0, 2, 1).reshape(ROWS, FEAT).astype(jnp.bfloat16)
    dest = destination[:, 0].astype(jnp.int32)
    wall_index = jnp.arange(ROWS, dtype=jnp.int32) // S % N_WALL
    shard = dest * N_WALL + wall_index
    counts = jax.ops.segment_sum(jnp.ones((ROWS,), jnp.float32), shard, num_segments=devices_all)
    row_scale = 1.0 / counts[shard]
    onehot = (dest.reshape(devices_all, S, 1) == jnp.arange(N_SPAN, dtype=jnp.int32)[None, None, :]).astype(jnp.int32)
    slots = lax.optimization_barrier(jnp.sum((jnp.cumsum(onehot, axis=1) - 1) * onehot, axis=2)).reshape(ROWS).astype(jnp.int32)
    place = jnp.arange(ROWS, dtype=jnp.int32) // S * CAP + slots
    slot_total = devices_all * CAP
    targets_f = targets

    def station(carry, xs):
        station_weights = xs[:5]
        station_index = xs[5]
        where_to = jnp.where(dest == station_index, place, slot_total).astype(jnp.int32)
        in_rows = jnp.zeros((slot_total, FEAT), jnp.bfloat16).at[where_to].set(rows, mode='drop')
        in_targets = jnp.zeros((slot_total, OUT), jnp.bfloat16).at[where_to].set(targets_f, mode='drop')
        in_scale = jnp.zeros((slot_total,), jnp.float32).at[where_to].set(row_scale, mode='drop')
        grads = row_grads(in_rows, in_targets, in_scale, station_weights)
        return (carry, grads)
    xs = (weight_in, weight_two, weight_three, weight_four, weight_out, jnp.arange(N_SPAN, dtype=jnp.int32))
    unused_carry, grads = lax.scan(station, jnp.zeros((), jnp.int32), xs)
    return (new_field, grads[0], grads[1], grads[2], grads[3], grads[4])
```

```python
import math

import jax
import jax.numpy as jnp
from jax import lax
from jax.sharding import PartitionSpec as P

P_SIZE = 5
S = 128
FEAT = 128


step_scale = 0.04


def extended(x, sides, width):
    for axis, dim in sides:
        size, length = (lax.axis_size(axis), x.shape[dim])
        up = [(i, (i + 1) % size) for i in range(size - 1)]
        down = [(j, i) for i, j in up]
        last = lax.slice_in_dim(x, length - width, length, axis=dim)
        first = lax.slice_in_dim(x, 0, width, axis=dim)
        before = lax.ppermute(last, axis, up)
        after = lax.ppermute(first, axis, down)
        x = jnp.concatenate([before, x, after], axis=dim)
    return x


def legendre_pair(order, point):
    value_prev = 1.0
    value_now = point
    slope_prev = 0.0
    slope_now = 1.0
    for degree in range(1, order):
        value_next = ((2 * degree + 1) * point * value_now - degree * value_prev) / (degree + 1)
        slope_next = slope_prev + (2 * degree + 1) * value_now
        value_prev, value_now = (value_now, value_next)
        slope_prev, slope_now = (slope_now, slope_next)
    return (value_now, slope_now)


def gauss_nodes(count):
    found = []
    for index in range(count):
        guess = math.cos(math.pi * (index + 0.75) / (count + 0.5))
        for sweep in range(60):
            value, slope = legendre_pair(count, guess)
            guess = guess - value / slope
        found.append(guess)
    return sorted(found)


def fr_tables():
    nodes = gauss_nodes(P_SIZE)
    bary = []
    for j in range(P_SIZE):
        product = 1.0
        for m in range(P_SIZE):
            if m != j:
                product = product * (nodes[j] - nodes[m])
        bary.append(1.0 / product)
    deriv = [[0.0] * P_SIZE for row_index in range(P_SIZE)]
    for i in range(P_SIZE):
        for j in range(P_SIZE):
            if i != j:
                deriv[i][j] = bary[j] / bary[i] / (nodes[i] - nodes[j])
        deriv[i][i] = -sum((deriv[i][j] for j in range(P_SIZE) if j != i))

    def basis_at(point):
        values = []
        for j in range(P_SIZE):
            product = 1.0
            for m in range(P_SIZE):
                if m != j:
                    product = product * (point - nodes[m]) / (nodes[j] - nodes[m])
            values.append(product)
        return values

    left_value = basis_at(-1.0)
    right_value = basis_at(1.0)
    sign = (-1.0) ** P_SIZE
    slope_left = [
        0.5 * sign * (legendre_pair(P_SIZE, x)[1] - legendre_pair(P_SIZE - 1, x)[1]) for x in nodes
    ]
    slope_right = [-slope_left[P_SIZE - 1 - i] for i in range(P_SIZE)]
    return tuple(
        (
            jnp.asarray(table, jnp.float32)
            for table in (deriv, left_value, right_value, slope_left, slope_right)
        )
    )


def along(matrix, field, axis):
    return jnp.moveaxis(
        jnp.tensordot(matrix, field, axes=([1], [axis]), precision=lax.Precision.HIGHEST), 0, axis
    )


def at_face(vector, field, axis):
    return jnp.tensordot(vector, field, axes=([0], [axis]), precision=lax.Precision.HIGHEST)


def spread(face, vector, axis, ndim):
    target_shape = [1] * ndim
    target_shape[axis] = vector.shape[0]
    return jnp.expand_dims(face, axis) * vector.reshape(target_shape)


def upwind(state_before, speed_before, state_after, speed_after):
    mean_speed = 0.5 * (speed_before + speed_after)
    return 0.5 * mean_speed * (state_before + state_after) - 0.5 * jnp.abs(mean_speed) * (
        state_after - state_before
    )


def face_states(field, speed, axis, tables):
    left_value = tables[1]
    right_value = tables[2]
    return (
        at_face(left_value, field, axis),
        at_face(left_value, speed, axis),
        at_face(right_value, field, axis),
        at_face(right_value, speed, axis),
    )


def divergence(field, speed, axis, own, before, after, tables):
    deriv, left_value, right_value, slope_left, slope_right = tables
    flux = speed * field
    volume = along(deriv, flux, axis)
    flux_left = at_face(left_value, flux, axis)
    flux_right = at_face(right_value, flux, axis)
    common_left = upwind(before[0], before[1], own[0], own[1])
    common_right = upwind(own[2], own[3], after[0], after[1])
    return (
        volume
        + spread(common_left - flux_left, slope_left, axis, field.ndim)
        + spread(common_right - flux_right, slope_right, axis, field.ndim)
    )


def forward(inputs, weights):
    acts = [inputs]
    pres = []
    hidden = inputs
    for layer in weights[:-1]:
        pre = jnp.dot(hidden, layer, preferred_element_type=jnp.float32)
        pres.append(pre)
        hidden = jax.nn.silu(pre).astype(jnp.bfloat16)
        acts.append(hidden)
    return (jnp.dot(hidden, weights[-1], preferred_element_type=jnp.float32), acts, pres)


def backward_layer(error, weight, pre):
    back = lax.dot_general(
        error, weight, (((1,), (1,)), ((), ())), preferred_element_type=jnp.float32
    )
    sigma = jax.nn.sigmoid(pre)
    return (back * sigma * (1.0 + pre * (1.0 - sigma))).astype(jnp.bfloat16)


def weight_grad(act, error):
    return lax.dot_general(act, error, (((0,), (0,)), ((), ())), preferred_element_type=jnp.float32)


def neighbour_faces(direction, field, speed, tables):
    count = field.shape[3 + direction]
    face_axis = 3 + direction
    stacked = jnp.stack([field, speed])
    if direction == 0:
        padded = extended(stacked, (("span", 4),), 1)
    else:
        padded = extended(stacked, (("wall", 5),), 1)
    padded_left = at_face(tables[1], padded, 1 + direction)
    padded_right = at_face(tables[2], padded, 1 + direction)
    before = lax.slice_in_dim(padded_right, 0, count, axis=face_axis)
    after = lax.slice_in_dim(padded_left, 2, count + 2, axis=face_axis)
    return ((before[0], before[1]), (after[0], after[1]))


def local(
    field,
    velocity,
    cells,
    destination,
    targets,
    weight_in,
    weight_two,
    weight_three,
    weight_four,
    weight_out,
):
    tables = fr_tables()
    total = jnp.zeros_like(field)
    for direction in range(3):
        speed = velocity[direction]
        own = face_states(field, speed, direction, tables)
        if direction < 2:
            before, after = neighbour_faces(direction, field, speed, tables)
        else:
            before = (jnp.roll(own[2], 1, 4), jnp.roll(own[3], 1, 4))
            after = (jnp.roll(own[0], -1, 4), jnp.roll(own[1], -1, 4))
        total = total + divergence(field, speed, direction, own, before, after, tables)
    new_field = field - step_scale * total
    local_count = field.shape[3] * field.shape[4] * field.shape[5]
    speed_means = jnp.mean(velocity.reshape(3, P_SIZE * P_SIZE * P_SIZE, local_count), axis=1)
    values = jnp.concatenate(
        [new_field.reshape(P_SIZE * P_SIZE * P_SIZE, local_count), speed_means], axis=0
    )
    rows = jnp.take(values, cells, axis=1).T.astype(jnp.bfloat16)
    span_count = lax.axis_size("span")
    slot_count = S // 8
    dest = destination[:, 0]
    onehot = (dest[:, None] == jnp.arange(span_count, dtype=jnp.int32)[None, :]).astype(jnp.int32)
    slots = jnp.sum((jnp.cumsum(onehot, axis=0) - 1) * onehot, axis=1)
    position = dest * slot_count + slots
    out_width = targets.shape[1]
    flag_block = jnp.zeros((rows.shape[0], 128), jnp.bfloat16).at[:, 0].set(1.0)
    payload = jnp.concatenate([rows, targets, flag_block], axis=1)
    width = payload.shape[1]
    buffer = jnp.zeros((span_count * slot_count, width), jnp.bfloat16).at[position].set(payload)
    got = lax.all_to_all(
        buffer.reshape(span_count, slot_count, width), "span", split_axis=0, concat_axis=0, tiled=True
    ).reshape(span_count * slot_count, width)
    inputs = got[:, :FEAT]
    wanted = got[:, FEAT : FEAT + out_width].astype(jnp.float32)
    flags = got[:, FEAT + out_width].astype(jnp.float32)
    row_scale = flags / jnp.maximum(jnp.sum(flags), 1.0)
    layer_one = weight_in[0]
    layer_two = weight_two[0]
    layer_three = weight_three[0]
    layer_four = weight_four[0]
    layer_last = weight_out[0]
    weights = (layer_one, layer_two, layer_three, layer_four, layer_last)
    output, acts, pres = forward(inputs, weights)
    error = (row_scale[:, None] * (output - wanted)).astype(jnp.bfloat16)
    grad_last = weight_grad(acts[4], error)
    error = backward_layer(error, layer_last, pres[3])
    grad_fourth = weight_grad(acts[3], error)
    error = backward_layer(error, layer_four, pres[2])
    grad_third = weight_grad(acts[2], error)
    error = backward_layer(error, layer_three, pres[1])
    grad_second = weight_grad(acts[1], error)
    error = backward_layer(error, layer_two, pres[0])
    grad_first = weight_grad(acts[0], error)
    grads = (grad_first, grad_second, grad_third, grad_fourth, grad_last)
    summed = wall_sum(grads)
    return (new_field,) + tuple(g[None] for g in summed)


def wall_sum(grads):
    size = lax.axis_size("wall")
    bits = size.bit_length() - 1
    if (1 << bits) != size:
        return lax.psum(grads, "wall")
    lanes = 128
    flat = jnp.concatenate([g.reshape(-1, lanes) for g in grads], axis=0)
    me = lax.axis_index("wall")
    for bit in range(bits):
        mine = (me >> bit) & 1
        halves = flat.reshape(2, flat.shape[0] // 2, lanes)
        keep = lax.dynamic_index_in_dim(halves, mine, 0, keepdims=False)
        send = lax.dynamic_index_in_dim(halves, 1 - mine, 0, keepdims=False)
        pairs = [(i, i ^ (1 << bit)) for i in range(size)]
        flat = keep + lax.ppermute(send, "wall", pairs)
    for bit in reversed(range(bits)):
        mine = (me >> bit) & 1
        pairs = [(i, i ^ (1 << bit)) for i in range(size)]
        other = lax.ppermute(flat, "wall", pairs)
        low = jnp.where(mine == 0, flat, other)
        high = jnp.where(mine == 0, other, flat)
        flat = jnp.concatenate([low, high], axis=0)
    out = []
    at = 0
    for g in grads:
        rows_of = g.size // lanes
        out.append(flat[at : at + rows_of].reshape(g.shape))
        at += rows_of
    return tuple(out)


def solution(mesh):
    in_specs = (
        P(None, None, None, "span", "wall", None),
        P(None, None, None, None, "span", "wall", None),
        P(("span", "wall")),
        P(("span", "wall"), None),
        P(("span", "wall"), None),
        P("span", None, None),
        P("span", None, None),
        P("span", None, None),
        P("span", None, None),
        P("span", None, None),
    )
    out_specs = (
        P(None, None, None, "span", "wall", None),
        P("span", None, None),
        P("span", None, None),
        P("span", None, None),
        P("span", None, None),
        P("span", None, None),
    )
    return jax.shard_map(local, mesh=mesh, in_specs=in_specs, out_specs=out_specs, check_vma=False)
```

```python
import math

import jax
import jax.numpy as jnp
from jax import lax
from jax.sharding import PartitionSpec as P

P_SIZE = 5
S = 128
FEAT = 128


step_scale = 0.04
EMPTY_MARK = 1024.0


def extended(x, sides, width):
    for axis, dim in sides:
        size, length = (lax.axis_size(axis), x.shape[dim])
        up = [(i, (i + 1) % size) for i in range(size - 1)]
        down = [(j, i) for i, j in up]
        last = lax.slice_in_dim(x, length - width, length, axis=dim)
        first = lax.slice_in_dim(x, 0, width, axis=dim)
        before = lax.ppermute(last, axis, up)
        after = lax.ppermute(first, axis, down)
        x = jnp.concatenate([before, x, after], axis=dim)
    return x


def legendre_pair(order, point):
    value_prev = 1.0
    value_now = point
    slope_prev = 0.0
    slope_now = 1.0
    for degree in range(1, order):
        value_next = ((2 * degree + 1) * point * value_now - degree * value_prev) / (degree + 1)
        slope_next = slope_prev + (2 * degree + 1) * value_now
        value_prev, value_now = (value_now, value_next)
        slope_prev, slope_now = (slope_now, slope_next)
    return (value_now, slope_now)


def gauss_nodes(count):
    found = []
    for index in range(count):
        guess = math.cos(math.pi * (index + 0.75) / (count + 0.5))
        for sweep in range(60):
            value, slope = legendre_pair(count, guess)
            guess = guess - value / slope
        found.append(guess)
    return sorted(found)


def fr_tables():
    nodes = gauss_nodes(P_SIZE)
    bary = []
    for j in range(P_SIZE):
        product = 1.0
        for m in range(P_SIZE):
            if m != j:
                product = product * (nodes[j] - nodes[m])
        bary.append(1.0 / product)
    deriv = [[0.0] * P_SIZE for row_index in range(P_SIZE)]
    for i in range(P_SIZE):
        for j in range(P_SIZE):
            if i != j:
                deriv[i][j] = bary[j] / bary[i] / (nodes[i] - nodes[j])
        deriv[i][i] = -sum((deriv[i][j] for j in range(P_SIZE) if j != i))

    def basis_at(point):
        values = []
        for j in range(P_SIZE):
            product = 1.0
            for m in range(P_SIZE):
                if m != j:
                    product = product * (point - nodes[m]) / (nodes[j] - nodes[m])
            values.append(product)
        return values

    left_value = basis_at(-1.0)
    right_value = basis_at(1.0)
    sign = (-1.0) ** P_SIZE
    slope_left = [
        0.5 * sign * (legendre_pair(P_SIZE, x)[1] - legendre_pair(P_SIZE - 1, x)[1]) for x in nodes
    ]
    slope_right = [-slope_left[P_SIZE - 1 - i] for i in range(P_SIZE)]
    return tuple(
        (
            jnp.asarray(table, jnp.float32)
            for table in (deriv, left_value, right_value, slope_left, slope_right)
        )
    )


def along(matrix, field, axis):
    return jnp.moveaxis(
        jnp.tensordot(matrix, field, axes=([1], [axis]), precision=lax.Precision.HIGHEST), 0, axis
    )


def at_face(vector, field, axis):
    return jnp.tensordot(vector, field, axes=([0], [axis]), precision=lax.Precision.HIGHEST)


def spread(face, vector, axis, ndim):
    target_shape = [1] * ndim
    target_shape[axis] = vector.shape[0]
    return jnp.expand_dims(face, axis) * vector.reshape(target_shape)


def upwind(state_before, speed_before, state_after, speed_after):
    mean_speed = 0.5 * (speed_before + speed_after)
    return 0.5 * mean_speed * (state_before + state_after) - 0.5 * jnp.abs(mean_speed) * (
        state_after - state_before
    )


def face_states(field, speed, axis, tables):
    left_value = tables[1]
    right_value = tables[2]
    return (
        at_face(left_value, field, axis),
        at_face(left_value, speed, axis),
        at_face(right_value, field, axis),
        at_face(right_value, speed, axis),
    )


def divergence(field, speed, axis, own, before, after, tables):
    deriv, left_value, right_value, slope_left, slope_right = tables
    flux = speed * field
    volume = along(deriv, flux, axis)
    flux_left = at_face(left_value, flux, axis)
    flux_right = at_face(right_value, flux, axis)
    common_left = upwind(before[0], before[1], own[0], own[1])
    common_right = upwind(own[2], own[3], after[0], after[1])
    return (
        volume
        + spread(common_left - flux_left, slope_left, axis, field.ndim)
        + spread(common_right - flux_right, slope_right, axis, field.ndim)
    )


def forward(inputs, weights):
    acts = [inputs]
    pres = []
    hidden = inputs
    for layer in weights[:-1]:
        pre = jnp.dot(hidden, layer, preferred_element_type=jnp.float32)
        pres.append(pre)
        hidden = jax.nn.silu(pre).astype(jnp.bfloat16)
        acts.append(hidden)
    return (jnp.dot(hidden, weights[-1], preferred_element_type=jnp.float32), acts, pres)


def backward_layer(error, weight, pre):
    back = lax.dot_general(
        error, weight, (((1,), (1,)), ((), ())), preferred_element_type=jnp.float32
    )
    sigma = jax.nn.sigmoid(pre)
    return (back * sigma * (1.0 + pre * (1.0 - sigma))).astype(jnp.bfloat16)


def weight_grad(act, error):
    return lax.dot_general(act, error, (((0,), (0,)), ((), ())), preferred_element_type=jnp.float32)


def neighbour_faces(direction, field, speed, tables):
    count = field.shape[3 + direction]
    face_axis = 3 + direction
    stacked = jnp.stack([field, speed])
    if direction == 0:
        padded = extended(stacked, (("span", 4),), 1)
    else:
        padded = extended(stacked, (("wall", 5),), 1)
    padded_left = at_face(tables[1], padded, 1 + direction)
    padded_right = at_face(tables[2], padded, 1 + direction)
    before = lax.slice_in_dim(padded_right, 0, count, axis=face_axis)
    after = lax.slice_in_dim(padded_left, 2, count + 2, axis=face_axis)
    return ((before[0], before[1]), (after[0], after[1]))


def local(
    field,
    velocity,
    cells,
    destination,
    targets,
    weight_in,
    weight_two,
    weight_three,
    weight_four,
    weight_out,
):
    tables = fr_tables()
    total = jnp.zeros_like(field)
    for direction in range(3):
        speed = velocity[direction]
        own = face_states(field, speed, direction, tables)
        if direction < 2:
            before, after = neighbour_faces(direction, field, speed, tables)
        else:
            before = (jnp.roll(own[2], 1, 4), jnp.roll(own[3], 1, 4))
            after = (jnp.roll(own[0], -1, 4), jnp.roll(own[1], -1, 4))
        total = total + divergence(field, speed, direction, own, before, after, tables)
    new_field = field - step_scale * total
    local_count = field.shape[3] * field.shape[4] * field.shape[5]
    speed_means = jnp.mean(velocity.reshape(3, P_SIZE * P_SIZE * P_SIZE, local_count), axis=1)
    values = jnp.concatenate(
        [new_field.reshape(P_SIZE * P_SIZE * P_SIZE, local_count), speed_means], axis=0
    )
    rows = jnp.take(values, cells, axis=1).T.astype(jnp.bfloat16)
    span_count = lax.axis_size("span")
    slot_count = S // 8
    dest = destination[:, 0]
    onehot = (dest[:, None] == jnp.arange(span_count, dtype=jnp.int32)[None, :]).astype(jnp.int32)
    slots = jnp.sum((jnp.cumsum(onehot, axis=0) - 1) * onehot, axis=1)
    position = dest * slot_count + slots
    out_width = targets.shape[1]
    payload = jnp.concatenate([rows, targets], axis=1)
    width = payload.shape[1]
    empty = jnp.concatenate(
        [jnp.zeros((1, FEAT), jnp.bfloat16), jnp.full((1, out_width), EMPTY_MARK, jnp.bfloat16)], axis=1
    )
    buffer = jnp.broadcast_to(empty, (span_count * slot_count, width)).at[position].set(payload)
    got = lax.all_to_all(
        buffer.reshape(span_count, slot_count, width), "span", split_axis=0, concat_axis=0, tiled=True
    ).reshape(span_count * slot_count, width)
    inputs = got[:, :FEAT]
    wanted_raw = got[:, FEAT : FEAT + out_width].astype(jnp.float32)
    filled = wanted_raw[:, :1] < EMPTY_MARK / 2
    wanted = jnp.where(filled, wanted_raw, 0.0)
    flags = filled[:, 0].astype(jnp.float32)
    row_scale = flags / jnp.maximum(jnp.sum(flags), 1.0)
    layer_one = weight_in[0]
    layer_two = weight_two[0]
    layer_three = weight_three[0]
    layer_four = weight_four[0]
    layer_last = weight_out[0]
    weights = (layer_one, layer_two, layer_three, layer_four, layer_last)
    output, acts, pres = forward(inputs, weights)
    error = (row_scale[:, None] * (output - wanted)).astype(jnp.bfloat16)
    grad_last = weight_grad(acts[4], error)
    error = backward_layer(error, layer_last, pres[3])
    grad_fourth = weight_grad(acts[3], error)
    error = backward_layer(error, layer_four, pres[2])
    grad_third = weight_grad(acts[2], error)
    error = backward_layer(error, layer_three, pres[1])
    grad_second = weight_grad(acts[1], error)
    error = backward_layer(error, layer_two, pres[0])
    grad_first = weight_grad(acts[0], error)
    grads = (grad_first, grad_second, grad_third, grad_fourth, grad_last)
    summed = wall_sum(grads)
    return (new_field,) + tuple(g[None] for g in summed)


def wall_sum(grads):
    size = lax.axis_size("wall")
    bits = size.bit_length() - 1
    if (1 << bits) != size:
        return lax.psum(grads, "wall")
    lanes = 128
    flat = jnp.concatenate([g.reshape(-1, lanes) for g in grads], axis=0)
    me = lax.axis_index("wall")
    split_bits = min(3, bits)
    for bit in range(split_bits):
        mine = (me >> bit) & 1
        halves = flat.reshape(2, flat.shape[0] // 2, lanes)
        keep = lax.dynamic_index_in_dim(halves, mine, 0, keepdims=False)
        send = lax.dynamic_index_in_dim(halves, 1 - mine, 0, keepdims=False)
        pairs = [(i, i ^ (1 << bit)) for i in range(size)]
        flat = keep + lax.ppermute(send, "wall", pairs)
    for bit in range(split_bits, bits):
        pairs = [(i, i ^ (1 << bit)) for i in range(size)]
        flat = flat + lax.ppermute(flat, "wall", pairs)
    for bit in reversed(range(split_bits)):
        mine = (me >> bit) & 1
        pairs = [(i, i ^ (1 << bit)) for i in range(size)]
        other = lax.ppermute(flat, "wall", pairs)
        low = jnp.where(mine == 0, flat, other)
        high = jnp.where(mine == 0, other, flat)
        flat = jnp.concatenate([low, high], axis=0)
    out = []
    at = 0
    for g in grads:
        rows_of = g.size // lanes
        out.append(flat[at : at + rows_of].reshape(g.shape))
        at += rows_of
    return tuple(out)


def solution(mesh):
    in_specs = (
        P(None, None, None, "span", "wall", None),
        P(None, None, None, None, "span", "wall", None),
        P(("span", "wall")),
        P(("span", "wall"), None),
        P(("span", "wall"), None),
        P("span", None, None),
        P("span", None, None),
        P("span", None, None),
        P("span", None, None),
        P("span", None, None),
    )
    out_specs = (
        P(None, None, None, "span", "wall", None),
        P("span", None, None),
        P("span", None, None),
        P("span", None, None),
        P("span", None, None),
        P("span", None, None),
    )
    return jax.shard_map(local, mesh=mesh, in_specs=in_specs, out_specs=out_specs, check_vma=False)
```

```python
import math

import jax
import jax.numpy as jnp
from jax import lax
from jax.sharding import PartitionSpec as P

P_SIZE = 5
S = 128
FEAT = 128


step_scale = 0.04
EMPTY_MARK = 1024.0


def extended(x, sides, width):
    for axis, dim in sides:
        size, length = (lax.axis_size(axis), x.shape[dim])
        up = [(i, (i + 1) % size) for i in range(size - 1)]
        down = [(j, i) for i, j in up]
        last = lax.slice_in_dim(x, length - width, length, axis=dim)
        first = lax.slice_in_dim(x, 0, width, axis=dim)
        before = lax.ppermute(last, axis, up)
        after = lax.ppermute(first, axis, down)
        x = jnp.concatenate([before, x, after], axis=dim)
    return x


def legendre_pair(order, point):
    value_prev = 1.0
    value_now = point
    slope_prev = 0.0
    slope_now = 1.0
    for degree in range(1, order):
        value_next = ((2 * degree + 1) * point * value_now - degree * value_prev) / (degree + 1)
        slope_next = slope_prev + (2 * degree + 1) * value_now
        value_prev, value_now = (value_now, value_next)
        slope_prev, slope_now = (slope_now, slope_next)
    return (value_now, slope_now)


def gauss_nodes(count):
    found = []
    for index in range(count):
        guess = math.cos(math.pi * (index + 0.75) / (count + 0.5))
        for sweep in range(60):
            value, slope = legendre_pair(count, guess)
            guess = guess - value / slope
        found.append(guess)
    return sorted(found)


def fr_tables():
    nodes = gauss_nodes(P_SIZE)
    bary = []
    for j in range(P_SIZE):
        product = 1.0
        for m in range(P_SIZE):
            if m != j:
                product = product * (nodes[j] - nodes[m])
        bary.append(1.0 / product)
    deriv = [[0.0] * P_SIZE for row_index in range(P_SIZE)]
    for i in range(P_SIZE):
        for j in range(P_SIZE):
            if i != j:
                deriv[i][j] = bary[j] / bary[i] / (nodes[i] - nodes[j])
        deriv[i][i] = -sum((deriv[i][j] for j in range(P_SIZE) if j != i))

    def basis_at(point):
        values = []
        for j in range(P_SIZE):
            product = 1.0
            for m in range(P_SIZE):
                if m != j:
                    product = product * (point - nodes[m]) / (nodes[j] - nodes[m])
            values.append(product)
        return values

    left_value = basis_at(-1.0)
    right_value = basis_at(1.0)
    sign = (-1.0) ** P_SIZE
    slope_left = [
        0.5 * sign * (legendre_pair(P_SIZE, x)[1] - legendre_pair(P_SIZE - 1, x)[1]) for x in nodes
    ]
    slope_right = [-slope_left[P_SIZE - 1 - i] for i in range(P_SIZE)]
    return tuple(
        (
            jnp.asarray(table, jnp.float32)
            for table in (deriv, left_value, right_value, slope_left, slope_right)
        )
    )


def along(matrix, field, axis):
    return jnp.moveaxis(
        jnp.tensordot(matrix, field, axes=([1], [axis]), precision=lax.Precision.HIGHEST), 0, axis
    )


def at_face(vector, field, axis):
    return jnp.tensordot(vector, field, axes=([0], [axis]), precision=lax.Precision.HIGHEST)


def spread(face, vector, axis, ndim):
    target_shape = [1] * ndim
    target_shape[axis] = vector.shape[0]
    return jnp.expand_dims(face, axis) * vector.reshape(target_shape)


def upwind(state_before, speed_before, state_after, speed_after):
    mean_speed = 0.5 * (speed_before + speed_after)
    return 0.5 * mean_speed * (state_before + state_after) - 0.5 * jnp.abs(mean_speed) * (
        state_after - state_before
    )


def face_states(field, speed, axis, tables):
    left_value = tables[1]
    right_value = tables[2]
    return (
        at_face(left_value, field, axis),
        at_face(left_value, speed, axis),
        at_face(right_value, field, axis),
        at_face(right_value, speed, axis),
    )


def divergence(field, speed, axis, own, before, after, tables):
    deriv, left_value, right_value, slope_left, slope_right = tables
    flux = speed * field
    volume = along(deriv, flux, axis)
    flux_left = at_face(left_value, flux, axis)
    flux_right = at_face(right_value, flux, axis)
    common_left = upwind(before[0], before[1], own[0], own[1])
    common_right = upwind(own[2], own[3], after[0], after[1])
    return (
        volume
        + spread(common_left - flux_left, slope_left, axis, field.ndim)
        + spread(common_right - flux_right, slope_right, axis, field.ndim)
    )


def forward(inputs, weights):
    acts = [inputs]
    pres = []
    hidden = inputs
    for layer in weights[:-1]:
        pre = jnp.dot(hidden, layer, preferred_element_type=jnp.float32)
        pres.append(pre)
        hidden = jax.nn.silu(pre).astype(jnp.bfloat16)
        acts.append(hidden)
    return (jnp.dot(hidden, weights[-1], preferred_element_type=jnp.float32), acts, pres)


def backward_layer(error, weight, pre):
    back = lax.dot_general(
        error, weight, (((1,), (1,)), ((), ())), preferred_element_type=jnp.float32
    )
    sigma = jax.nn.sigmoid(pre)
    return (back * sigma * (1.0 + pre * (1.0 - sigma))).astype(jnp.bfloat16)


def weight_grad(act, error):
    return lax.dot_general(act, error, (((0,), (0,)), ((), ())), preferred_element_type=jnp.float32)


def neighbour_faces(direction, field, speed, tables):
    count = field.shape[3 + direction]
    face_axis = 3 + direction
    stacked = jnp.stack([field, speed])
    if direction == 0:
        padded = extended(stacked, (("span", 4),), 1)
    else:
        padded = extended(stacked, (("wall", 5),), 1)
    padded_left = at_face(tables[1], padded, 1 + direction)
    padded_right = at_face(tables[2], padded, 1 + direction)
    before = lax.slice_in_dim(padded_right, 0, count, axis=face_axis)
    after = lax.slice_in_dim(padded_left, 2, count + 2, axis=face_axis)
    return ((before[0], before[1]), (after[0], after[1]))


def local(
    field,
    velocity,
    cells,
    destination,
    targets,
    weight_in,
    weight_two,
    weight_three,
    weight_four,
    weight_out,
):
    tables = fr_tables()
    total = jnp.zeros_like(field)
    for direction in range(3):
        speed = velocity[direction]
        own = face_states(field, speed, direction, tables)
        if direction < 2:
            before, after = neighbour_faces(direction, field, speed, tables)
        else:
            before = (jnp.roll(own[2], 1, 4), jnp.roll(own[3], 1, 4))
            after = (jnp.roll(own[0], -1, 4), jnp.roll(own[1], -1, 4))
        total = total + divergence(field, speed, direction, own, before, after, tables)
    new_field = field - step_scale * total
    local_count = field.shape[3] * field.shape[4] * field.shape[5]
    speed_means = jnp.mean(velocity.reshape(3, P_SIZE * P_SIZE * P_SIZE, local_count), axis=1)
    values = jnp.concatenate(
        [new_field.reshape(P_SIZE * P_SIZE * P_SIZE, local_count), speed_means], axis=0
    )
    rows = jnp.take(values, cells, axis=1).T.astype(jnp.bfloat16)
    span_count = lax.axis_size("span")
    slot_count = S // 8
    dest = destination[:, 0]
    onehot = (dest[:, None] == jnp.arange(span_count, dtype=jnp.int32)[None, :]).astype(jnp.int32)
    slots = jnp.sum((jnp.cumsum(onehot, axis=0) - 1) * onehot, axis=1)
    position = dest * slot_count + slots
    out_width = targets.shape[1]
    payload = jnp.concatenate([rows, targets], axis=1)
    width = payload.shape[1]
    empty = jnp.concatenate(
        [jnp.zeros((1, FEAT), jnp.bfloat16), jnp.full((1, out_width), EMPTY_MARK, jnp.bfloat16)], axis=1
    )
    buffer = jnp.broadcast_to(empty, (span_count * slot_count, width)).at[position].set(payload)
    got = lax.all_to_all(
        buffer.reshape(span_count, slot_count, width), "span", split_axis=0, concat_axis=0, tiled=True
    ).reshape(span_count * slot_count, width)
    inputs = got[:, :FEAT]
    wanted_raw = got[:, FEAT : FEAT + out_width].astype(jnp.float32)
    filled = wanted_raw[:, :1] < EMPTY_MARK / 2
    wanted = jnp.where(filled, wanted_raw, 0.0)
    flags = filled[:, 0].astype(jnp.float32)
    row_scale = flags / jnp.maximum(jnp.sum(flags), 1.0)
    layer_one = weight_in[0]
    layer_two = weight_two[0]
    layer_three = weight_three[0]
    layer_four = weight_four[0]
    layer_last = weight_out[0]
    weights = (layer_one, layer_two, layer_three, layer_four, layer_last)
    output, acts, pres = forward(inputs, weights)
    error = (row_scale[:, None] * (output - wanted)).astype(jnp.bfloat16)
    grad_last = weight_grad(acts[4], error)
    error = backward_layer(error, layer_last, pres[3])
    grad_fourth = weight_grad(acts[3], error)
    error = backward_layer(error, layer_four, pres[2])
    grad_third = weight_grad(acts[2], error)
    error = backward_layer(error, layer_three, pres[1])
    grad_second = weight_grad(acts[1], error)
    error = backward_layer(error, layer_two, pres[0])
    grad_first = weight_grad(acts[0], error)
    grads = (grad_first, grad_second, grad_third, grad_fourth, grad_last)
    summed = wall_sum(grads)
    return (new_field,) + tuple(g[None] for g in summed)


def wall_sum(grads):
    size = lax.axis_size("wall")
    groups = wall_groups(size)
    if groups is None:
        return lax.psum(grads, "wall")
    lanes = 128
    flat = jnp.concatenate([g.reshape(-1, lanes) for g in grads], axis=0)
    me = lax.axis_index("wall")
    scatter_groups = [(off, count) for off, count in groups if count > 2]
    exchange_groups = [(off, count) for off, count in groups if count <= 2]
    for off, count in scatter_groups:
        coord = (me >> off) & (count - 1)
        parts = flat.reshape(count, flat.shape[0] // count, lanes)
        total = lax.dynamic_index_in_dim(parts, coord, 0, keepdims=False)
        for shift in range(1, count):
            send = lax.dynamic_index_in_dim(parts, (coord + shift) % count, 0, keepdims=False)
            total = total + lax.ppermute(send, "wall", group_pairs(size, off, count, shift))
        flat = total
    for off, count in exchange_groups:
        flat = flat + lax.ppermute(flat, "wall", group_pairs(size, off, count, 1))
    for off, count in reversed(scatter_groups):
        coord = (me >> off) & (count - 1)
        got = [flat] + [
            lax.ppermute(flat, "wall", group_pairs(size, off, count, shift)) for shift in range(1, count)
        ]
        stacked = jnp.stack(got)
        flat = jnp.concatenate(
            [
                lax.dynamic_index_in_dim(stacked, (coord - part) % count, 0, keepdims=False)
                for part in range(count)
            ],
            axis=0,
        )
    out = []
    at = 0
    for g in grads:
        rows_of = g.size // lanes
        out.append(flat[at : at + rows_of].reshape(g.shape))
        at += rows_of
    return tuple(out)


def wall_groups(size):
    if size != 32:
        return None
    return [(0, 4), (2, 4), (4, 2)]


def group_pairs(size, off, count, shift):
    pairs = []
    for i in range(size):
        coord = (i >> off) & (count - 1)
        dest = i - (coord << off) + (((coord + shift) % count) << off)
        pairs.append((i, dest))
    return pairs


def solution(mesh):
    in_specs = (
        P(None, None, None, "span", "wall", None),
        P(None, None, None, None, "span", "wall", None),
        P(("span", "wall")),
        P(("span", "wall"), None),
        P(("span", "wall"), None),
        P("span", None, None),
        P("span", None, None),
        P("span", None, None),
        P("span", None, None),
        P("span", None, None),
    )
    out_specs = (
        P(None, None, None, "span", "wall", None),
        P("span", None, None),
        P("span", None, None),
        P("span", None, None),
        P("span", None, None),
        P("span", None, None),
    )
    return jax.shard_map(local, mesh=mesh, in_specs=in_specs, out_specs=out_specs, check_vma=False)
```

```python
import math

import jax
import jax.numpy as jnp
from jax import lax
from jax.sharding import PartitionSpec as P

P_SIZE = 5
S = 128
FEAT = 128


step_scale = 0.04
EMPTY_MARK = 1024.0


def extended(x, sides, width):
    for axis, dim in sides:
        size, length = (lax.axis_size(axis), x.shape[dim])
        up = [(i, (i + 1) % size) for i in range(size - 1)]
        down = [(j, i) for i, j in up]
        last = lax.slice_in_dim(x, length - width, length, axis=dim)
        first = lax.slice_in_dim(x, 0, width, axis=dim)
        before = lax.ppermute(last, axis, up)
        after = lax.ppermute(first, axis, down)
        x = jnp.concatenate([before, x, after], axis=dim)
    return x


def legendre_pair(order, point):
    value_prev = 1.0
    value_now = point
    slope_prev = 0.0
    slope_now = 1.0
    for degree in range(1, order):
        value_next = ((2 * degree + 1) * point * value_now - degree * value_prev) / (degree + 1)
        slope_next = slope_prev + (2 * degree + 1) * value_now
        value_prev, value_now = (value_now, value_next)
        slope_prev, slope_now = (slope_now, slope_next)
    return (value_now, slope_now)


def gauss_nodes(count):
    found = []
    for index in range(count):
        guess = math.cos(math.pi * (index + 0.75) / (count + 0.5))
        for sweep in range(60):
            value, slope = legendre_pair(count, guess)
            guess = guess - value / slope
        found.append(guess)
    return sorted(found)


def fr_tables():
    nodes = gauss_nodes(P_SIZE)
    bary = []
    for j in range(P_SIZE):
        product = 1.0
        for m in range(P_SIZE):
            if m != j:
                product = product * (nodes[j] - nodes[m])
        bary.append(1.0 / product)
    deriv = [[0.0] * P_SIZE for row_index in range(P_SIZE)]
    for i in range(P_SIZE):
        for j in range(P_SIZE):
            if i != j:
                deriv[i][j] = bary[j] / bary[i] / (nodes[i] - nodes[j])
        deriv[i][i] = -sum((deriv[i][j] for j in range(P_SIZE) if j != i))

    def basis_at(point):
        values = []
        for j in range(P_SIZE):
            product = 1.0
            for m in range(P_SIZE):
                if m != j:
                    product = product * (point - nodes[m]) / (nodes[j] - nodes[m])
            values.append(product)
        return values

    left_value = basis_at(-1.0)
    right_value = basis_at(1.0)
    sign = (-1.0) ** P_SIZE
    slope_left = [
        0.5 * sign * (legendre_pair(P_SIZE, x)[1] - legendre_pair(P_SIZE - 1, x)[1]) for x in nodes
    ]
    slope_right = [-slope_left[P_SIZE - 1 - i] for i in range(P_SIZE)]
    return tuple(
        (
            jnp.asarray(table, jnp.float32)
            for table in (deriv, left_value, right_value, slope_left, slope_right)
        )
    )


def along(matrix, field, axis):
    return jnp.moveaxis(
        jnp.tensordot(matrix, field, axes=([1], [axis]), precision=lax.Precision.HIGHEST), 0, axis
    )


def at_face(vector, field, axis):
    return jnp.tensordot(vector, field, axes=([0], [axis]), precision=lax.Precision.HIGHEST)


def spread(face, vector, axis, ndim):
    target_shape = [1] * ndim
    target_shape[axis] = vector.shape[0]
    return jnp.expand_dims(face, axis) * vector.reshape(target_shape)


def upwind(state_before, speed_before, state_after, speed_after):
    mean_speed = 0.5 * (speed_before + speed_after)
    return 0.5 * mean_speed * (state_before + state_after) - 0.5 * jnp.abs(mean_speed) * (
        state_after - state_before
    )


def face_states(field, speed, axis, tables):
    left_value = tables[1]
    right_value = tables[2]
    return (
        at_face(left_value, field, axis),
        at_face(left_value, speed, axis),
        at_face(right_value, field, axis),
        at_face(right_value, speed, axis),
    )


def divergence(field, speed, axis, own, before, after, tables):
    deriv, left_value, right_value, slope_left, slope_right = tables
    flux = speed * field
    volume = along(deriv, flux, axis)
    flux_left = at_face(left_value, flux, axis)
    flux_right = at_face(right_value, flux, axis)
    common_left = upwind(before[0], before[1], own[0], own[1])
    common_right = upwind(own[2], own[3], after[0], after[1])
    return (
        volume
        + spread(common_left - flux_left, slope_left, axis, field.ndim)
        + spread(common_right - flux_right, slope_right, axis, field.ndim)
    )


def forward(inputs, weights):
    acts = [inputs]
    pres = []
    hidden = inputs
    for layer in weights[:-1]:
        pre = jnp.dot(hidden, layer, preferred_element_type=jnp.float32)
        pres.append(pre)
        hidden = jax.nn.silu(pre).astype(jnp.bfloat16)
        acts.append(hidden)
    return (jnp.dot(hidden, weights[-1], preferred_element_type=jnp.float32), acts, pres)


def backward_layer(error, weight, pre):
    back = lax.dot_general(
        error, weight, (((1,), (1,)), ((), ())), preferred_element_type=jnp.float32
    )
    sigma = jax.nn.sigmoid(pre)
    return (back * sigma * (1.0 + pre * (1.0 - sigma))).astype(jnp.bfloat16)


def weight_grad(act, error):
    return lax.dot_general(act, error, (((0,), (0,)), ((), ())), preferred_element_type=jnp.float32)


def neighbour_faces(direction, field, speed, tables):
    count = field.shape[3 + direction]
    face_axis = 3 + direction
    stacked = jnp.stack([field, speed])
    if direction == 0:
        padded = extended(stacked, (("span", 4),), 1)
    else:
        padded = extended(stacked, (("wall", 5),), 1)
    padded_left = at_face(tables[1], padded, 1 + direction)
    padded_right = at_face(tables[2], padded, 1 + direction)
    before = lax.slice_in_dim(padded_right, 0, count, axis=face_axis)
    after = lax.slice_in_dim(padded_left, 2, count + 2, axis=face_axis)
    return ((before[0], before[1]), (after[0], after[1]))


def local(
    field,
    velocity,
    cells,
    destination,
    targets,
    weight_in,
    weight_two,
    weight_three,
    weight_four,
    weight_out,
):
    tables = fr_tables()
    total = jnp.zeros_like(field)
    for direction in range(3):
        speed = velocity[direction]
        own = face_states(field, speed, direction, tables)
        if direction < 2:
            before, after = neighbour_faces(direction, field, speed, tables)
        else:
            before = (jnp.roll(own[2], 1, 4), jnp.roll(own[3], 1, 4))
            after = (jnp.roll(own[0], -1, 4), jnp.roll(own[1], -1, 4))
        total = total + divergence(field, speed, direction, own, before, after, tables)
    new_field = field - step_scale * total
    local_count = field.shape[3] * field.shape[4] * field.shape[5]
    speed_means = jnp.mean(velocity.reshape(3, P_SIZE * P_SIZE * P_SIZE, local_count), axis=1)
    values = jnp.concatenate(
        [new_field.reshape(P_SIZE * P_SIZE * P_SIZE, local_count), speed_means], axis=0
    )
    rows = jnp.take(values, cells, axis=1).T.astype(jnp.bfloat16)
    span_count = lax.axis_size("span")
    slot_count = S // 8
    dest = destination[:, 0]
    onehot = (dest[:, None] == jnp.arange(span_count, dtype=jnp.int32)[None, :]).astype(jnp.int32)
    slots = jnp.sum((jnp.cumsum(onehot, axis=0) - 1) * onehot, axis=1)
    position = dest * slot_count + slots
    out_width = targets.shape[1]
    payload = jnp.concatenate([rows, targets], axis=1)
    width = payload.shape[1]
    empty = jnp.concatenate(
        [jnp.zeros((1, FEAT), jnp.bfloat16), jnp.full((1, out_width), EMPTY_MARK, jnp.bfloat16)], axis=1
    )
    buffer = jnp.broadcast_to(empty, (span_count * slot_count, width)).at[position].set(payload)
    got = lax.all_to_all(
        buffer.reshape(span_count, slot_count, width), "span", split_axis=0, concat_axis=0, tiled=True
    ).reshape(span_count * slot_count, width)
    inputs = got[:, :FEAT]
    wanted_raw = got[:, FEAT : FEAT + out_width].astype(jnp.float32)
    filled = wanted_raw[:, :1] < EMPTY_MARK / 2
    wanted = jnp.where(filled, wanted_raw, 0.0)
    flags = filled[:, 0].astype(jnp.float32)
    row_scale = flags / jnp.maximum(jnp.sum(flags), 1.0)
    layer_one = weight_in[0]
    layer_two = weight_two[0]
    layer_three = weight_three[0]
    layer_four = weight_four[0]
    layer_last = weight_out[0]
    weights = (layer_one, layer_two, layer_three, layer_four, layer_last)
    output, acts, pres = forward(inputs, weights)
    error = (row_scale[:, None] * (output - wanted)).astype(jnp.bfloat16)
    grad_last = weight_grad(acts[4], error)
    error = backward_layer(error, layer_last, pres[3])
    grad_fourth = weight_grad(acts[3], error)
    error = backward_layer(error, layer_four, pres[2])
    grad_third = weight_grad(acts[2], error)
    error = backward_layer(error, layer_three, pres[1])
    grad_second = weight_grad(acts[1], error)
    error = backward_layer(error, layer_two, pres[0])
    grad_first = weight_grad(acts[0], error)
    grads = (grad_first, grad_second, grad_third, grad_fourth, grad_last)
    summed = wall_sum(grads)
    return (new_field,) + tuple(g[None] for g in summed)


def wall_sum(grads):
    size = lax.axis_size("wall")
    groups = wall_groups(size)
    if groups is None:
        return lax.psum(grads, "wall")
    lanes = 128
    flat = jnp.concatenate([g.reshape(-1, lanes) for g in grads], axis=0)
    me = lax.axis_index("wall")
    scatter_groups = [(off, count) for off, count in groups if count > 2]
    exchange_groups = [(off, count) for off, count in groups if count <= 2]
    for off, count in scatter_groups:
        coord = (me >> off) & (count - 1)
        parts = flat.reshape(count, flat.shape[0] // count, lanes)
        total = lax.dynamic_index_in_dim(parts, coord, 0, keepdims=False)
        for shift in range(1, count):
            send = lax.dynamic_index_in_dim(parts, (coord + shift) % count, 0, keepdims=False)
            total = total + lax.ppermute(send, "wall", group_pairs(size, off, count, shift))
        flat = total
    for off, count in exchange_groups:
        flat = flat + lax.ppermute(flat, "wall", group_pairs(size, off, count, 1))
    for off, count in reversed(scatter_groups):
        coord = (me >> off) & (count - 1)
        got = [flat] + [
            lax.ppermute(flat, "wall", group_pairs(size, off, count, shift)) for shift in range(1, count)
        ]
        stacked = jnp.stack(got)
        flat = jnp.concatenate(
            [
                lax.dynamic_index_in_dim(stacked, (coord - part) % count, 0, keepdims=False)
                for part in range(count)
            ],
            axis=0,
        )
    out = []
    at = 0
    for g in grads:
        rows_of = g.size // lanes
        out.append(flat[at : at + rows_of].reshape(g.shape))
        at += rows_of
    return tuple(out)


def wall_groups(size):
    if size != 32:
        return None
    return [(0, 16), (4, 2)]


def group_pairs(size, off, count, shift):
    pairs = []
    for i in range(size):
        coord = (i >> off) & (count - 1)
        dest = i - (coord << off) + (((coord + shift) % count) << off)
        pairs.append((i, dest))
    return pairs


def solution(mesh):
    in_specs = (
        P(None, None, None, "span", "wall", None),
        P(None, None, None, None, "span", "wall", None),
        P(("span", "wall")),
        P(("span", "wall"), None),
        P(("span", "wall"), None),
        P("span", None, None),
        P("span", None, None),
        P("span", None, None),
        P("span", None, None),
        P("span", None, None),
    )
    out_specs = (
        P(None, None, None, "span", "wall", None),
        P("span", None, None),
        P("span", None, None),
        P("span", None, None),
        P("span", None, None),
        P("span", None, None),
    )
    return jax.shard_map(local, mesh=mesh, in_specs=in_specs, out_specs=out_specs, check_vma=False)
```

```python
import math

import jax
import jax.numpy as jnp
from jax import lax
from jax.sharding import PartitionSpec as P

P_SIZE = 5
S = 128
FEAT = 128


step_scale = 0.04
EMPTY_MARK = 1024.0


def extended(x, sides, width):
    for axis, dim in sides:
        size, length = (lax.axis_size(axis), x.shape[dim])
        up = [(i, (i + 1) % size) for i in range(size - 1)]
        down = [(j, i) for i, j in up]
        last = lax.slice_in_dim(x, length - width, length, axis=dim)
        first = lax.slice_in_dim(x, 0, width, axis=dim)
        before = lax.ppermute(last, axis, up)
        after = lax.ppermute(first, axis, down)
        x = jnp.concatenate([before, x, after], axis=dim)
    return x


def legendre_pair(order, point):
    value_prev = 1.0
    value_now = point
    slope_prev = 0.0
    slope_now = 1.0
    for degree in range(1, order):
        value_next = ((2 * degree + 1) * point * value_now - degree * value_prev) / (degree + 1)
        slope_next = slope_prev + (2 * degree + 1) * value_now
        value_prev, value_now = (value_now, value_next)
        slope_prev, slope_now = (slope_now, slope_next)
    return (value_now, slope_now)


def gauss_nodes(count):
    found = []
    for index in range(count):
        guess = math.cos(math.pi * (index + 0.75) / (count + 0.5))
        for sweep in range(60):
            value, slope = legendre_pair(count, guess)
            guess = guess - value / slope
        found.append(guess)
    return sorted(found)


def fr_tables():
    nodes = gauss_nodes(P_SIZE)
    bary = []
    for j in range(P_SIZE):
        product = 1.0
        for m in range(P_SIZE):
            if m != j:
                product = product * (nodes[j] - nodes[m])
        bary.append(1.0 / product)
    deriv = [[0.0] * P_SIZE for row_index in range(P_SIZE)]
    for i in range(P_SIZE):
        for j in range(P_SIZE):
            if i != j:
                deriv[i][j] = bary[j] / bary[i] / (nodes[i] - nodes[j])
        deriv[i][i] = -sum((deriv[i][j] for j in range(P_SIZE) if j != i))

    def basis_at(point):
        values = []
        for j in range(P_SIZE):
            product = 1.0
            for m in range(P_SIZE):
                if m != j:
                    product = product * (point - nodes[m]) / (nodes[j] - nodes[m])
            values.append(product)
        return values

    left_value = basis_at(-1.0)
    right_value = basis_at(1.0)
    sign = (-1.0) ** P_SIZE
    slope_left = [
        0.5 * sign * (legendre_pair(P_SIZE, x)[1] - legendre_pair(P_SIZE - 1, x)[1]) for x in nodes
    ]
    slope_right = [-slope_left[P_SIZE - 1 - i] for i in range(P_SIZE)]
    return tuple(
        (
            jnp.asarray(table, jnp.float32)
            for table in (deriv, left_value, right_value, slope_left, slope_right)
        )
    )


def along(matrix, field, axis):
    return jnp.moveaxis(
        jnp.tensordot(matrix, field, axes=([1], [axis]), precision=lax.Precision.HIGHEST), 0, axis
    )


def at_face(vector, field, axis):
    return jnp.tensordot(vector, field, axes=([0], [axis]), precision=lax.Precision.HIGHEST)


def spread(face, vector, axis, ndim):
    target_shape = [1] * ndim
    target_shape[axis] = vector.shape[0]
    return jnp.expand_dims(face, axis) * vector.reshape(target_shape)


def upwind(state_before, speed_before, state_after, speed_after):
    mean_speed = 0.5 * (speed_before + speed_after)
    return 0.5 * mean_speed * (state_before + state_after) - 0.5 * jnp.abs(mean_speed) * (
        state_after - state_before
    )


def face_states(field, speed, axis, tables):
    left_value = tables[1]
    right_value = tables[2]
    return (
        at_face(left_value, field, axis),
        at_face(left_value, speed, axis),
        at_face(right_value, field, axis),
        at_face(right_value, speed, axis),
    )


def divergence(field, speed, axis, own, before, after, tables):
    deriv, left_value, right_value, slope_left, slope_right = tables
    flux = speed * field
    volume = along(deriv, flux, axis)
    flux_left = at_face(left_value, flux, axis)
    flux_right = at_face(right_value, flux, axis)
    common_left = upwind(before[0], before[1], own[0], own[1])
    common_right = upwind(own[2], own[3], after[0], after[1])
    return (
        volume
        + spread(common_left - flux_left, slope_left, axis, field.ndim)
        + spread(common_right - flux_right, slope_right, axis, field.ndim)
    )


def forward(inputs, weights):
    acts = [inputs]
    pres = []
    hidden = inputs
    for layer in weights[:-1]:
        pre = jnp.dot(hidden, layer, preferred_element_type=jnp.float32)
        pres.append(pre)
        hidden = jax.nn.silu(pre).astype(jnp.bfloat16)
        acts.append(hidden)
    return (jnp.dot(hidden, weights[-1], preferred_element_type=jnp.float32), acts, pres)


def backward_layer(error, weight, pre):
    back = lax.dot_general(
        error, weight, (((1,), (1,)), ((), ())), preferred_element_type=jnp.float32
    )
    sigma = jax.nn.sigmoid(pre)
    return (back * sigma * (1.0 + pre * (1.0 - sigma))).astype(jnp.bfloat16)


def weight_grad(act, error):
    return lax.dot_general(act, error, (((0,), (0,)), ((), ())), preferred_element_type=jnp.float32)


def neighbour_faces(direction, field, speed, tables):
    count = field.shape[3 + direction]
    face_axis = 3 + direction
    stacked = jnp.stack([field, speed])
    if direction == 0:
        padded = extended(stacked, (("span", 4),), 1)
    else:
        padded = extended(stacked, (("wall", 5),), 1)
    padded_left = at_face(tables[1], padded, 1 + direction)
    padded_right = at_face(tables[2], padded, 1 + direction)
    before = lax.slice_in_dim(padded_right, 0, count, axis=face_axis)
    after = lax.slice_in_dim(padded_left, 2, count + 2, axis=face_axis)
    return ((before[0], before[1]), (after[0], after[1]))


def local(
    field,
    velocity,
    cells,
    destination,
    targets,
    weight_in,
    weight_two,
    weight_three,
    weight_four,
    weight_out,
):
    tables = fr_tables()
    total = jnp.zeros_like(field)
    for direction in range(3):
        speed = velocity[direction]
        own = face_states(field, speed, direction, tables)
        if direction < 2:
            before, after = neighbour_faces(direction, field, speed, tables)
        else:
            before = (jnp.roll(own[2], 1, 4), jnp.roll(own[3], 1, 4))
            after = (jnp.roll(own[0], -1, 4), jnp.roll(own[1], -1, 4))
        total = total + divergence(field, speed, direction, own, before, after, tables)
    new_field = field - step_scale * total
    local_count = field.shape[3] * field.shape[4] * field.shape[5]
    speed_means = jnp.mean(velocity.reshape(3, P_SIZE * P_SIZE * P_SIZE, local_count), axis=1)
    values = jnp.concatenate(
        [new_field.reshape(P_SIZE * P_SIZE * P_SIZE, local_count), speed_means], axis=0
    )
    rows = jnp.take(values, cells, axis=1).T.astype(jnp.bfloat16)
    span_count = lax.axis_size("span")
    slot_count = S // 8
    dest = destination[:, 0]
    onehot = (dest[:, None] == jnp.arange(span_count, dtype=jnp.int32)[None, :]).astype(jnp.int32)
    slots = jnp.sum((jnp.cumsum(onehot, axis=0) - 1) * onehot, axis=1)
    position = dest * slot_count + slots
    out_width = targets.shape[1]
    target_buffer = (
        jnp.full((span_count * slot_count, out_width), EMPTY_MARK, jnp.bfloat16).at[position].set(targets)
    )
    got_targets = lax.all_to_all(
        target_buffer.reshape(span_count, slot_count, out_width), "span", split_axis=0, concat_axis=0, tiled=True
    ).reshape(span_count * slot_count, out_width)
    row_buffer = jnp.zeros((span_count * slot_count, FEAT), jnp.bfloat16).at[position].set(rows)
    inputs = lax.all_to_all(
        row_buffer.reshape(span_count, slot_count, FEAT), "span", split_axis=0, concat_axis=0, tiled=True
    ).reshape(span_count * slot_count, FEAT)
    wanted_raw = got_targets.astype(jnp.float32)
    filled = wanted_raw[:, :1] < EMPTY_MARK / 2
    wanted = jnp.where(filled, wanted_raw, 0.0)
    flags = filled[:, 0].astype(jnp.float32)
    row_scale = flags / jnp.maximum(jnp.sum(flags), 1.0)
    layer_one = weight_in[0]
    layer_two = weight_two[0]
    layer_three = weight_three[0]
    layer_four = weight_four[0]
    layer_last = weight_out[0]
    weights = (layer_one, layer_two, layer_three, layer_four, layer_last)
    output, acts, pres = forward(inputs, weights)
    error = (row_scale[:, None] * (output - wanted)).astype(jnp.bfloat16)
    grad_last = weight_grad(acts[4], error)
    error = backward_layer(error, layer_last, pres[3])
    grad_fourth = weight_grad(acts[3], error)
    error = backward_layer(error, layer_four, pres[2])
    grad_third = weight_grad(acts[2], error)
    error = backward_layer(error, layer_three, pres[1])
    grad_second = weight_grad(acts[1], error)
    error = backward_layer(error, layer_two, pres[0])
    grad_first = weight_grad(acts[0], error)
    grads = (grad_first, grad_second, grad_third, grad_fourth, grad_last)
    summed = wall_sum(grads)
    return (new_field,) + tuple(g[None] for g in summed)


def wall_sum(grads):
    size = lax.axis_size("wall")
    groups = wall_groups(size)
    if groups is None:
        return lax.psum(grads, "wall")
    lanes = 128
    flat = jnp.concatenate([g.reshape(-1, lanes) for g in grads], axis=0)
    me = lax.axis_index("wall")
    scatter_groups = [(off, count) for off, count in groups if count > 2]
    exchange_groups = [(off, count) for off, count in groups if count <= 2]
    for off, count in scatter_groups:
        coord = (me >> off) & (count - 1)
        parts = flat.reshape(count, flat.shape[0] // count, lanes)
        total = lax.dynamic_index_in_dim(parts, coord, 0, keepdims=False)
        for shift in range(1, count):
            send = lax.dynamic_index_in_dim(parts, (coord + shift) % count, 0, keepdims=False)
            total = total + lax.ppermute(send, "wall", group_pairs(size, off, count, shift))
        flat = total
    for off, count in exchange_groups:
        flat = flat + lax.ppermute(flat, "wall", group_pairs(size, off, count, 1))
    for off, count in reversed(scatter_groups):
        coord = (me >> off) & (count - 1)
        got = [flat] + [
            lax.ppermute(flat, "wall", group_pairs(size, off, count, shift)) for shift in range(1, count)
        ]
        stacked = jnp.stack(got)
        flat = jnp.concatenate(
            [
                lax.dynamic_index_in_dim(stacked, (coord - part) % count, 0, keepdims=False)
                for part in range(count)
            ],
            axis=0,
        )
    out = []
    at = 0
    for g in grads:
        rows_of = g.size // lanes
        out.append(flat[at : at + rows_of].reshape(g.shape))
        at += rows_of
    return tuple(out)


def wall_groups(size):
    if size != 32:
        return None
    return [(0, 4), (2, 4), (4, 2)]


def group_pairs(size, off, count, shift):
    pairs = []
    for i in range(size):
        coord = (i >> off) & (count - 1)
        dest = i - (coord << off) + (((coord + shift) % count) << off)
        pairs.append((i, dest))
    return pairs


def solution(mesh):
    in_specs = (
        P(None, None, None, "span", "wall", None),
        P(None, None, None, None, "span", "wall", None),
        P(("span", "wall")),
        P(("span", "wall"), None),
        P(("span", "wall"), None),
        P("span", None, None),
        P("span", None, None),
        P("span", None, None),
        P("span", None, None),
        P("span", None, None),
    )
    out_specs = (
        P(None, None, None, "span", "wall", None),
        P("span", None, None),
        P("span", None, None),
        P("span", None, None),
        P("span", None, None),
        P("span", None, None),
    )
    return jax.shard_map(local, mesh=mesh, in_specs=in_specs, out_specs=out_specs, check_vma=False)
```

```python
import math

import jax
import jax.numpy as jnp
from jax import lax
from jax.sharding import PartitionSpec as P

P_SIZE = 5
S = 128
FEAT = 128


step_scale = 0.04
EMPTY_MARK = 1024.0


def extended(x, sides, width):
    for axis, dim in sides:
        size, length = (lax.axis_size(axis), x.shape[dim])
        up = [(i, (i + 1) % size) for i in range(size - 1)]
        down = [(j, i) for i, j in up]
        last = lax.slice_in_dim(x, length - width, length, axis=dim)
        first = lax.slice_in_dim(x, 0, width, axis=dim)
        before = lax.ppermute(last, axis, up)
        after = lax.ppermute(first, axis, down)
        x = jnp.concatenate([before, x, after], axis=dim)
    return x


def legendre_pair(order, point):
    value_prev = 1.0
    value_now = point
    slope_prev = 0.0
    slope_now = 1.0
    for degree in range(1, order):
        value_next = ((2 * degree + 1) * point * value_now - degree * value_prev) / (degree + 1)
        slope_next = slope_prev + (2 * degree + 1) * value_now
        value_prev, value_now = (value_now, value_next)
        slope_prev, slope_now = (slope_now, slope_next)
    return (value_now, slope_now)


def gauss_nodes(count):
    found = []
    for index in range(count):
        guess = math.cos(math.pi * (index + 0.75) / (count + 0.5))
        for sweep in range(60):
            value, slope = legendre_pair(count, guess)
            guess = guess - value / slope
        found.append(guess)
    return sorted(found)


def fr_tables():
    nodes = gauss_nodes(P_SIZE)
    bary = []
    for j in range(P_SIZE):
        product = 1.0
        for m in range(P_SIZE):
            if m != j:
                product = product * (nodes[j] - nodes[m])
        bary.append(1.0 / product)
    deriv = [[0.0] * P_SIZE for row_index in range(P_SIZE)]
    for i in range(P_SIZE):
        for j in range(P_SIZE):
            if i != j:
                deriv[i][j] = bary[j] / bary[i] / (nodes[i] - nodes[j])
        deriv[i][i] = -sum((deriv[i][j] for j in range(P_SIZE) if j != i))

    def basis_at(point):
        values = []
        for j in range(P_SIZE):
            product = 1.0
            for m in range(P_SIZE):
                if m != j:
                    product = product * (point - nodes[m]) / (nodes[j] - nodes[m])
            values.append(product)
        return values

    left_value = basis_at(-1.0)
    right_value = basis_at(1.0)
    sign = (-1.0) ** P_SIZE
    slope_left = [
        0.5 * sign * (legendre_pair(P_SIZE, x)[1] - legendre_pair(P_SIZE - 1, x)[1]) for x in nodes
    ]
    slope_right = [-slope_left[P_SIZE - 1 - i] for i in range(P_SIZE)]
    return tuple(
        (
            jnp.asarray(table, jnp.float32)
            for table in (deriv, left_value, right_value, slope_left, slope_right)
        )
    )


def along(matrix, field, axis):
    return jnp.moveaxis(
        jnp.tensordot(matrix, field, axes=([1], [axis]), precision=lax.Precision.HIGHEST), 0, axis
    )


def at_face(vector, field, axis):
    return jnp.tensordot(vector, field, axes=([0], [axis]), precision=lax.Precision.HIGHEST)


def spread(face, vector, axis, ndim):
    target_shape = [1] * ndim
    target_shape[axis] = vector.shape[0]
    return jnp.expand_dims(face, axis) * vector.reshape(target_shape)


def upwind(state_before, speed_before, state_after, speed_after):
    mean_speed = 0.5 * (speed_before + speed_after)
    return 0.5 * mean_speed * (state_before + state_after) - 0.5 * jnp.abs(mean_speed) * (
        state_after - state_before
    )


def face_states(field, speed, axis, tables):
    left_value = tables[1]
    right_value = tables[2]
    return (
        at_face(left_value, field, axis),
        at_face(left_value, speed, axis),
        at_face(right_value, field, axis),
        at_face(right_value, speed, axis),
    )


def divergence(field, speed, axis, own, before, after, tables):
    deriv, left_value, right_value, slope_left, slope_right = tables
    flux = speed * field
    volume = along(deriv, flux, axis)
    flux_left = at_face(left_value, flux, axis)
    flux_right = at_face(right_value, flux, axis)
    common_left = upwind(before[0], before[1], own[0], own[1])
    common_right = upwind(own[2], own[3], after[0], after[1])
    return (
        volume
        + spread(common_left - flux_left, slope_left, axis, field.ndim)
        + spread(common_right - flux_right, slope_right, axis, field.ndim)
    )


def forward(inputs, weights):
    acts = [inputs]
    pres = []
    hidden = inputs
    for layer in weights[:-1]:
        pre = jnp.dot(hidden, layer, preferred_element_type=jnp.float32)
        pres.append(pre)
        hidden = jax.nn.silu(pre).astype(jnp.bfloat16)
        acts.append(hidden)
    return (jnp.dot(hidden, weights[-1], preferred_element_type=jnp.float32), acts, pres)


def backward_layer(error, weight, pre):
    back = lax.dot_general(
        error, weight, (((1,), (1,)), ((), ())), preferred_element_type=jnp.float32
    )
    sigma = jax.nn.sigmoid(pre)
    return (back * sigma * (1.0 + pre * (1.0 - sigma))).astype(jnp.bfloat16)


def weight_grad(act, error):
    return lax.dot_general(act, error, (((0,), (0,)), ((), ())), preferred_element_type=jnp.float32)


def neighbour_faces(direction, field, speed, tables):
    count = field.shape[3 + direction]
    face_axis = 3 + direction
    stacked = jnp.stack([field, speed])
    own_left = at_face(tables[1], stacked, 1 + direction)
    own_right = at_face(tables[2], stacked, 1 + direction)
    axis = "span" if direction == 0 else "wall"
    padded_left = extended(own_left, ((axis, face_axis),), 1)
    padded_right = extended(own_right, ((axis, face_axis),), 1)
    before = lax.slice_in_dim(padded_right, 0, count, axis=face_axis)
    after = lax.slice_in_dim(padded_left, 2, count + 2, axis=face_axis)
    return ((before[0], before[1]), (after[0], after[1]))


def local(
    field,
    velocity,
    cells,
    destination,
    targets,
    weight_in,
    weight_two,
    weight_three,
    weight_four,
    weight_out,
):
    tables = fr_tables()
    total = jnp.zeros_like(field)
    for direction in range(3):
        speed = velocity[direction]
        own = face_states(field, speed, direction, tables)
        if direction < 2:
            before, after = neighbour_faces(direction, field, speed, tables)
        else:
            before = (jnp.roll(own[2], 1, 4), jnp.roll(own[3], 1, 4))
            after = (jnp.roll(own[0], -1, 4), jnp.roll(own[1], -1, 4))
        total = total + divergence(field, speed, direction, own, before, after, tables)
    new_field = field - step_scale * total
    local_count = field.shape[3] * field.shape[4] * field.shape[5]
    speed_means = jnp.mean(velocity.reshape(3, P_SIZE * P_SIZE * P_SIZE, local_count), axis=1)
    values = jnp.concatenate(
        [new_field.reshape(P_SIZE * P_SIZE * P_SIZE, local_count), speed_means], axis=0
    )
    rows = jnp.take(values, cells, axis=1).T.astype(jnp.bfloat16)
    span_count = lax.axis_size("span")
    slot_count = S // 8
    dest = destination[:, 0]
    onehot = (dest[:, None] == jnp.arange(span_count, dtype=jnp.int32)[None, :]).astype(jnp.int32)
    slots = jnp.sum((jnp.cumsum(onehot, axis=0) - 1) * onehot, axis=1)
    position = dest * slot_count + slots
    out_width = targets.shape[1]
    payload = jnp.concatenate([rows, targets], axis=1)
    width = payload.shape[1]
    empty = jnp.concatenate(
        [jnp.zeros((1, FEAT), jnp.bfloat16), jnp.full((1, out_width), EMPTY_MARK, jnp.bfloat16)], axis=1
    )
    buffer = jnp.broadcast_to(empty, (span_count * slot_count, width)).at[position].set(payload)
    got = lax.all_to_all(
        buffer.reshape(span_count, slot_count, width), "span", split_axis=0, concat_axis=0, tiled=True
    ).reshape(span_count * slot_count, width)
    inputs = got[:, :FEAT]
    wanted_raw = got[:, FEAT : FEAT + out_width].astype(jnp.float32)
    filled = wanted_raw[:, :1] < EMPTY_MARK / 2
    wanted = jnp.where(filled, wanted_raw, 0.0)
    flags = filled[:, 0].astype(jnp.float32)
    row_scale = flags / jnp.maximum(jnp.sum(flags), 1.0)
    layer_one = weight_in[0]
    layer_two = weight_two[0]
    layer_three = weight_three[0]
    layer_four = weight_four[0]
    layer_last = weight_out[0]
    weights = (layer_one, layer_two, layer_three, layer_four, layer_last)
    output, acts, pres = forward(inputs, weights)
    error = (row_scale[:, None] * (output - wanted)).astype(jnp.bfloat16)
    grad_last = weight_grad(acts[4], error)
    error = backward_layer(error, layer_last, pres[3])
    grad_fourth = weight_grad(acts[3], error)
    error = backward_layer(error, layer_four, pres[2])
    grad_third = weight_grad(acts[2], error)
    error = backward_layer(error, layer_three, pres[1])
    grad_second = weight_grad(acts[1], error)
    error = backward_layer(error, layer_two, pres[0])
    grad_first = weight_grad(acts[0], error)
    grads = (grad_first, grad_second, grad_third, grad_fourth, grad_last)
    summed = wall_sum(grads)
    return (new_field,) + tuple(g[None] for g in summed)


def wall_sum(grads):
    size = lax.axis_size("wall")
    groups = wall_groups(size)
    if groups is None:
        return lax.psum(grads, "wall")
    lanes = 128
    flat = jnp.concatenate([g.reshape(-1, lanes) for g in grads], axis=0)
    me = lax.axis_index("wall")
    scatter_groups = [(off, count) for off, count in groups if count > 2]
    exchange_groups = [(off, count) for off, count in groups if count <= 2]
    for off, count in scatter_groups:
        coord = (me >> off) & (count - 1)
        parts = flat.reshape(count, flat.shape[0] // count, lanes)
        total = lax.dynamic_index_in_dim(parts, coord, 0, keepdims=False)
        for shift in range(1, count):
            send = lax.dynamic_index_in_dim(parts, (coord + shift) % count, 0, keepdims=False)
            total = total + lax.ppermute(send, "wall", group_pairs(size, off, count, shift))
        flat = total
    for off, count in exchange_groups:
        flat = flat + lax.ppermute(flat, "wall", group_pairs(size, off, count, 1))
    for off, count in reversed(scatter_groups):
        coord = (me >> off) & (count - 1)
        got = [flat] + [
            lax.ppermute(flat, "wall", group_pairs(size, off, count, shift)) for shift in range(1, count)
        ]
        stacked = jnp.stack(got)
        flat = jnp.concatenate(
            [
                lax.dynamic_index_in_dim(stacked, (coord - part) % count, 0, keepdims=False)
                for part in range(count)
            ],
            axis=0,
        )
    out = []
    at = 0
    for g in grads:
        rows_of = g.size // lanes
        out.append(flat[at : at + rows_of].reshape(g.shape))
        at += rows_of
    return tuple(out)


def wall_groups(size):
    if size != 32:
        return None
    return [(0, 4), (2, 4), (4, 2)]


def group_pairs(size, off, count, shift):
    pairs = []
    for i in range(size):
        coord = (i >> off) & (count - 1)
        dest = i - (coord << off) + (((coord + shift) % count) << off)
        pairs.append((i, dest))
    return pairs


def solution(mesh):
    in_specs = (
        P(None, None, None, "span", "wall", None),
        P(None, None, None, None, "span", "wall", None),
        P(("span", "wall")),
        P(("span", "wall"), None),
        P(("span", "wall"), None),
        P("span", None, None),
        P("span", None, None),
        P("span", None, None),
        P("span", None, None),
        P("span", None, None),
    )
    out_specs = (
        P(None, None, None, "span", "wall", None),
        P("span", None, None),
        P("span", None, None),
        P("span", None, None),
        P("span", None, None),
        P("span", None, None),
    )
    return jax.shard_map(local, mesh=mesh, in_specs=in_specs, out_specs=out_specs, check_vma=False)
```

```python
import math

import jax
import jax.numpy as jnp
from jax import lax
from jax.sharding import PartitionSpec as P

P_SIZE = 5
S = 128
FEAT = 128


step_scale = 0.04
EMPTY_MARK = 1024.0
LINK_DTYPE = jnp.bfloat16


def extended(x, sides, width):
    for axis, dim in sides:
        size, length = (lax.axis_size(axis), x.shape[dim])
        up = [(i, (i + 1) % size) for i in range(size - 1)]
        down = [(j, i) for i, j in up]
        last = lax.slice_in_dim(x, length - width, length, axis=dim)
        first = lax.slice_in_dim(x, 0, width, axis=dim)
        before = lax.ppermute(last, axis, up)
        after = lax.ppermute(first, axis, down)
        x = jnp.concatenate([before, x, after], axis=dim)
    return x


def legendre_pair(order, point):
    value_prev = 1.0
    value_now = point
    slope_prev = 0.0
    slope_now = 1.0
    for degree in range(1, order):
        value_next = ((2 * degree + 1) * point * value_now - degree * value_prev) / (degree + 1)
        slope_next = slope_prev + (2 * degree + 1) * value_now
        value_prev, value_now = (value_now, value_next)
        slope_prev, slope_now = (slope_now, slope_next)
    return (value_now, slope_now)


def gauss_nodes(count):
    found = []
    for index in range(count):
        guess = math.cos(math.pi * (index + 0.75) / (count + 0.5))
        for sweep in range(60):
            value, slope = legendre_pair(count, guess)
            guess = guess - value / slope
        found.append(guess)
    return sorted(found)


def fr_tables():
    nodes = gauss_nodes(P_SIZE)
    bary = []
    for j in range(P_SIZE):
        product = 1.0
        for m in range(P_SIZE):
            if m != j:
                product = product * (nodes[j] - nodes[m])
        bary.append(1.0 / product)
    deriv = [[0.0] * P_SIZE for row_index in range(P_SIZE)]
    for i in range(P_SIZE):
        for j in range(P_SIZE):
            if i != j:
                deriv[i][j] = bary[j] / bary[i] / (nodes[i] - nodes[j])
        deriv[i][i] = -sum((deriv[i][j] for j in range(P_SIZE) if j != i))

    def basis_at(point):
        values = []
        for j in range(P_SIZE):
            product = 1.0
            for m in range(P_SIZE):
                if m != j:
                    product = product * (point - nodes[m]) / (nodes[j] - nodes[m])
            values.append(product)
        return values

    left_value = basis_at(-1.0)
    right_value = basis_at(1.0)
    sign = (-1.0) ** P_SIZE
    slope_left = [
        0.5 * sign * (legendre_pair(P_SIZE, x)[1] - legendre_pair(P_SIZE - 1, x)[1]) for x in nodes
    ]
    slope_right = [-slope_left[P_SIZE - 1 - i] for i in range(P_SIZE)]
    return tuple(
        (
            jnp.asarray(table, jnp.float32)
            for table in (deriv, left_value, right_value, slope_left, slope_right)
        )
    )


def along(matrix, field, axis):
    return jnp.moveaxis(
        jnp.tensordot(matrix, field, axes=([1], [axis]), precision=lax.Precision.HIGHEST), 0, axis
    )


def at_face(vector, field, axis):
    return jnp.tensordot(vector, field, axes=([0], [axis]), precision=lax.Precision.HIGHEST)


def spread(face, vector, axis, ndim):
    target_shape = [1] * ndim
    target_shape[axis] = vector.shape[0]
    return jnp.expand_dims(face, axis) * vector.reshape(target_shape)


def upwind(state_before, speed_before, state_after, speed_after):
    mean_speed = 0.5 * (speed_before + speed_after)
    return 0.5 * mean_speed * (state_before + state_after) - 0.5 * jnp.abs(mean_speed) * (
        state_after - state_before
    )


def face_states(field, speed, axis, tables):
    left_value = tables[1]
    right_value = tables[2]
    return (
        at_face(left_value, field, axis),
        at_face(left_value, speed, axis),
        at_face(right_value, field, axis),
        at_face(right_value, speed, axis),
    )


def divergence(field, speed, axis, own, before, after, tables):
    deriv, left_value, right_value, slope_left, slope_right = tables
    flux = speed * field
    volume = along(deriv, flux, axis)
    flux_left = at_face(left_value, flux, axis)
    flux_right = at_face(right_value, flux, axis)
    common_left = upwind(before[0], before[1], own[0], own[1])
    common_right = upwind(own[2], own[3], after[0], after[1])
    return (
        volume
        + spread(common_left - flux_left, slope_left, axis, field.ndim)
        + spread(common_right - flux_right, slope_right, axis, field.ndim)
    )


def forward(inputs, weights):
    acts = [inputs]
    pres = []
    hidden = inputs
    for layer in weights[:-1]:
        pre = jnp.dot(hidden, layer, preferred_element_type=jnp.float32)
        pres.append(pre)
        hidden = jax.nn.silu(pre).astype(jnp.bfloat16)
        acts.append(hidden)
    return (jnp.dot(hidden, weights[-1], preferred_element_type=jnp.float32), acts, pres)


def backward_layer(error, weight, pre):
    back = lax.dot_general(
        error, weight, (((1,), (1,)), ((), ())), preferred_element_type=jnp.float32
    )
    sigma = jax.nn.sigmoid(pre)
    return (back * sigma * (1.0 + pre * (1.0 - sigma))).astype(jnp.bfloat16)


def weight_grad(act, error):
    return lax.dot_general(act, error, (((0,), (0,)), ((), ())), preferred_element_type=jnp.float32)


def neighbour_faces(direction, field, speed, tables):
    count = field.shape[3 + direction]
    face_axis = 3 + direction
    stacked = jnp.stack([field, speed])
    own_left = at_face(tables[1], stacked, 1 + direction)
    own_right = at_face(tables[2], stacked, 1 + direction)
    axis = "span" if direction == 0 else "wall"
    padded_left = extended(own_left, ((axis, face_axis),), 1)
    padded_right = extended(own_right, ((axis, face_axis),), 1)
    before = lax.slice_in_dim(padded_right, 0, count, axis=face_axis)
    after = lax.slice_in_dim(padded_left, 2, count + 2, axis=face_axis)
    return ((before[0], before[1]), (after[0], after[1]))


def local(
    field,
    velocity,
    cells,
    destination,
    targets,
    weight_in,
    weight_two,
    weight_three,
    weight_four,
    weight_out,
):
    tables = fr_tables()
    total = jnp.zeros_like(field)
    for direction in range(3):
        speed = velocity[direction]
        own = face_states(field, speed, direction, tables)
        if direction < 2:
            before, after = neighbour_faces(direction, field, speed, tables)
        else:
            before = (jnp.roll(own[2], 1, 4), jnp.roll(own[3], 1, 4))
            after = (jnp.roll(own[0], -1, 4), jnp.roll(own[1], -1, 4))
        total = total + divergence(field, speed, direction, own, before, after, tables)
    new_field = field - step_scale * total
    local_count = field.shape[3] * field.shape[4] * field.shape[5]
    speed_means = jnp.mean(velocity.reshape(3, P_SIZE * P_SIZE * P_SIZE, local_count), axis=1)
    values = jnp.concatenate(
        [new_field.reshape(P_SIZE * P_SIZE * P_SIZE, local_count), speed_means], axis=0
    )
    rows = jnp.take(values, cells, axis=1).T.astype(jnp.bfloat16)
    span_count = lax.axis_size("span")
    slot_count = S // 8
    dest = destination[:, 0]
    onehot = (dest[:, None] == jnp.arange(span_count, dtype=jnp.int32)[None, :]).astype(jnp.int32)
    slots = jnp.sum((jnp.cumsum(onehot, axis=0) - 1) * onehot, axis=1)
    position = dest * slot_count + slots
    out_width = targets.shape[1]
    payload = jnp.concatenate([rows, targets], axis=1)
    width = payload.shape[1]
    empty = jnp.concatenate(
        [jnp.zeros((1, FEAT), jnp.bfloat16), jnp.full((1, out_width), EMPTY_MARK, jnp.bfloat16)], axis=1
    )
    buffer = jnp.broadcast_to(empty, (span_count * slot_count, width)).at[position].set(payload)
    got = lax.all_to_all(
        buffer.reshape(span_count, slot_count, width), "span", split_axis=0, concat_axis=0, tiled=True
    ).reshape(span_count * slot_count, width)
    inputs = got[:, :FEAT]
    wanted_raw = got[:, FEAT : FEAT + out_width].astype(jnp.float32)
    filled = wanted_raw[:, :1] < EMPTY_MARK / 2
    wanted = jnp.where(filled, wanted_raw, 0.0)
    flags = filled[:, 0].astype(jnp.float32)
    row_scale = flags / jnp.maximum(jnp.sum(flags), 1.0)
    layer_one = weight_in[0]
    layer_two = weight_two[0]
    layer_three = weight_three[0]
    layer_four = weight_four[0]
    layer_last = weight_out[0]
    weights = (layer_one, layer_two, layer_three, layer_four, layer_last)
    output, acts, pres = forward(inputs, weights)
    error = (row_scale[:, None] * (output - wanted)).astype(jnp.bfloat16)
    grad_last = weight_grad(acts[4], error)
    error = backward_layer(error, layer_last, pres[3])
    grad_fourth = weight_grad(acts[3], error)
    error = backward_layer(error, layer_four, pres[2])
    grad_third = weight_grad(acts[2], error)
    error = backward_layer(error, layer_three, pres[1])
    grad_second = weight_grad(acts[1], error)
    error = backward_layer(error, layer_two, pres[0])
    grad_first = weight_grad(acts[0], error)
    grads = (grad_first, grad_second, grad_third, grad_fourth, grad_last)
    summed = wall_sum(grads)
    return (new_field,) + tuple(g[None] for g in summed)


def wall_sum(grads):
    size = lax.axis_size("wall")
    groups = wall_groups(size)
    if groups is None:
        return lax.psum(grads, "wall")
    lanes = 128
    flat = jnp.concatenate([g.reshape(-1, lanes) for g in grads], axis=0)
    me = lax.axis_index("wall")
    scatter_groups = [(off, count) for off, count in groups if count > 2]
    exchange_groups = [(off, count) for off, count in groups if count <= 2]
    for off, count in scatter_groups:
        coord = (me >> off) & (count - 1)
        parts = flat.reshape(count, flat.shape[0] // count, lanes)
        total = lax.dynamic_index_in_dim(parts, coord, 0, keepdims=False)
        for shift in range(1, count):
            send = lax.dynamic_index_in_dim(parts, (coord + shift) % count, 0, keepdims=False)
            got = lax.ppermute(send.astype(LINK_DTYPE), "wall", group_pairs(size, off, count, shift))
            total = total + got.astype(jnp.float32)
        flat = total
    for off, count in exchange_groups:
        flat = flat + lax.ppermute(flat, "wall", group_pairs(size, off, count, 1))
    for off, count in reversed(scatter_groups):
        coord = (me >> off) & (count - 1)
        sent = flat.astype(LINK_DTYPE)
        got = [sent] + [
            lax.ppermute(sent, "wall", group_pairs(size, off, count, shift)) for shift in range(1, count)
        ]
        stacked = jnp.stack(got)
        flat = jnp.concatenate(
            [
                lax.dynamic_index_in_dim(stacked, (coord - part) % count, 0, keepdims=False)
                for part in range(count)
            ],
            axis=0,
        )
    flat = flat.astype(jnp.float32)
    out = []
    at = 0
    for g in grads:
        rows_of = g.size // lanes
        out.append(flat[at : at + rows_of].reshape(g.shape))
        at += rows_of
    return tuple(out)


def wall_groups(size):
    if size != 32:
        return None
    return [(0, 4), (2, 4), (4, 2)]


def group_pairs(size, off, count, shift):
    pairs = []
    for i in range(size):
        coord = (i >> off) & (count - 1)
        dest = i - (coord << off) + (((coord + shift) % count) << off)
        pairs.append((i, dest))
    return pairs


def solution(mesh):
    in_specs = (
        P(None, None, None, "span", "wall", None),
        P(None, None, None, None, "span", "wall", None),
        P(("span", "wall")),
        P(("span", "wall"), None),
        P(("span", "wall"), None),
        P("span", None, None),
        P("span", None, None),
        P("span", None, None),
        P("span", None, None),
        P("span", None, None),
    )
    out_specs = (
        P(None, None, None, "span", "wall", None),
        P("span", None, None),
        P("span", None, None),
        P("span", None, None),
        P("span", None, None),
        P("span", None, None),
    )
    return jax.shard_map(local, mesh=mesh, in_specs=in_specs, out_specs=out_specs, check_vma=False)
```

```python
import math

import jax
import jax.numpy as jnp
from jax import lax
from jax.sharding import PartitionSpec as P

P_SIZE = 5
S = 128
FEAT = 128


step_scale = 0.04
EMPTY_MARK = 1024.0
LINK_DTYPE = jnp.bfloat16


def extended(x, sides, width):
    for axis, dim in sides:
        size, length = (lax.axis_size(axis), x.shape[dim])
        up = [(i, (i + 1) % size) for i in range(size - 1)]
        down = [(j, i) for i, j in up]
        last = lax.slice_in_dim(x, length - width, length, axis=dim)
        first = lax.slice_in_dim(x, 0, width, axis=dim)
        before = lax.ppermute(last, axis, up)
        after = lax.ppermute(first, axis, down)
        x = jnp.concatenate([before, x, after], axis=dim)
    return x


def legendre_pair(order, point):
    value_prev = 1.0
    value_now = point
    slope_prev = 0.0
    slope_now = 1.0
    for degree in range(1, order):
        value_next = ((2 * degree + 1) * point * value_now - degree * value_prev) / (degree + 1)
        slope_next = slope_prev + (2 * degree + 1) * value_now
        value_prev, value_now = (value_now, value_next)
        slope_prev, slope_now = (slope_now, slope_next)
    return (value_now, slope_now)


def gauss_nodes(count):
    found = []
    for index in range(count):
        guess = math.cos(math.pi * (index + 0.75) / (count + 0.5))
        for sweep in range(60):
            value, slope = legendre_pair(count, guess)
            guess = guess - value / slope
        found.append(guess)
    return sorted(found)


def fr_tables():
    nodes = gauss_nodes(P_SIZE)
    bary = []
    for j in range(P_SIZE):
        product = 1.0
        for m in range(P_SIZE):
            if m != j:
                product = product * (nodes[j] - nodes[m])
        bary.append(1.0 / product)
    deriv = [[0.0] * P_SIZE for row_index in range(P_SIZE)]
    for i in range(P_SIZE):
        for j in range(P_SIZE):
            if i != j:
                deriv[i][j] = bary[j] / bary[i] / (nodes[i] - nodes[j])
        deriv[i][i] = -sum((deriv[i][j] for j in range(P_SIZE) if j != i))

    def basis_at(point):
        values = []
        for j in range(P_SIZE):
            product = 1.0
            for m in range(P_SIZE):
                if m != j:
                    product = product * (point - nodes[m]) / (nodes[j] - nodes[m])
            values.append(product)
        return values

    left_value = basis_at(-1.0)
    right_value = basis_at(1.0)
    sign = (-1.0) ** P_SIZE
    slope_left = [
        0.5 * sign * (legendre_pair(P_SIZE, x)[1] - legendre_pair(P_SIZE - 1, x)[1]) for x in nodes
    ]
    slope_right = [-slope_left[P_SIZE - 1 - i] for i in range(P_SIZE)]
    return tuple(
        (
            jnp.asarray(table, jnp.float32)
            for table in (deriv, left_value, right_value, slope_left, slope_right)
        )
    )


def along(matrix, field, axis):
    return jnp.moveaxis(
        jnp.tensordot(matrix, field, axes=([1], [axis]), precision=lax.Precision.HIGHEST), 0, axis
    )


def at_face(vector, field, axis):
    return jnp.tensordot(vector, field, axes=([0], [axis]), precision=lax.Precision.HIGHEST)


def spread(face, vector, axis, ndim):
    target_shape = [1] * ndim
    target_shape[axis] = vector.shape[0]
    return jnp.expand_dims(face, axis) * vector.reshape(target_shape)


def upwind(state_before, speed_before, state_after, speed_after):
    mean_speed = 0.5 * (speed_before + speed_after)
    return 0.5 * mean_speed * (state_before + state_after) - 0.5 * jnp.abs(mean_speed) * (
        state_after - state_before
    )


def face_states(field, speed, axis, tables):
    left_value = tables[1]
    right_value = tables[2]
    return (
        at_face(left_value, field, axis),
        at_face(left_value, speed, axis),
        at_face(right_value, field, axis),
        at_face(right_value, speed, axis),
    )


def divergence(field, speed, axis, own, before, after, tables):
    deriv, left_value, right_value, slope_left, slope_right = tables
    flux = speed * field
    volume = along(deriv, flux, axis)
    flux_left = at_face(left_value, flux, axis)
    flux_right = at_face(right_value, flux, axis)
    common_left = upwind(before[0], before[1], own[0], own[1])
    common_right = upwind(own[2], own[3], after[0], after[1])
    return (
        volume
        + spread(common_left - flux_left, slope_left, axis, field.ndim)
        + spread(common_right - flux_right, slope_right, axis, field.ndim)
    )


def forward(inputs, weights):
    acts = [inputs]
    pres = []
    hidden = inputs
    for layer in weights[:-1]:
        pre = jnp.dot(hidden, layer, preferred_element_type=jnp.float32)
        pres.append(pre)
        hidden = jax.nn.silu(pre).astype(jnp.bfloat16)
        acts.append(hidden)
    return (jnp.dot(hidden, weights[-1], preferred_element_type=jnp.float32), acts, pres)


def backward_layer(error, weight, pre):
    back = lax.dot_general(
        error, weight, (((1,), (1,)), ((), ())), preferred_element_type=jnp.float32
    )
    sigma = jax.nn.sigmoid(pre)
    return (back * sigma * (1.0 + pre * (1.0 - sigma))).astype(jnp.bfloat16)


def weight_grad(act, error):
    return lax.dot_general(act, error, (((0,), (0,)), ((), ())), preferred_element_type=jnp.float32)


def neighbour_faces(direction, field, speed, tables):
    count = field.shape[3 + direction]
    face_axis = 3 + direction
    stacked = jnp.stack([field, speed])
    own_left = at_face(tables[1], stacked, 1 + direction)
    own_right = at_face(tables[2], stacked, 1 + direction)
    axis = "span" if direction == 0 else "wall"
    padded_left = extended(own_left, ((axis, face_axis),), 1)
    padded_right = extended(own_right, ((axis, face_axis),), 1)
    before = lax.slice_in_dim(padded_right, 0, count, axis=face_axis)
    after = lax.slice_in_dim(padded_left, 2, count + 2, axis=face_axis)
    return ((before[0], before[1]), (after[0], after[1]))


def local(
    field,
    velocity,
    cells,
    destination,
    targets,
    weight_in,
    weight_two,
    weight_three,
    weight_four,
    weight_out,
):
    tables = fr_tables()
    total = jnp.zeros_like(field)
    for direction in range(3):
        speed = velocity[direction]
        own = face_states(field, speed, direction, tables)
        if direction < 2:
            before, after = neighbour_faces(direction, field, speed, tables)
        else:
            before = (jnp.roll(own[2], 1, 4), jnp.roll(own[3], 1, 4))
            after = (jnp.roll(own[0], -1, 4), jnp.roll(own[1], -1, 4))
        total = total + divergence(field, speed, direction, own, before, after, tables)
    new_field = field - step_scale * total
    local_count = field.shape[3] * field.shape[4] * field.shape[5]
    speed_means = jnp.mean(velocity.reshape(3, P_SIZE * P_SIZE * P_SIZE, local_count), axis=1)
    values = jnp.concatenate(
        [new_field.reshape(P_SIZE * P_SIZE * P_SIZE, local_count), speed_means], axis=0
    )
    rows = jnp.take(values, cells, axis=1).T.astype(jnp.bfloat16)
    span_count = lax.axis_size("span")
    slot_count = S // 8
    dest = destination[:, 0]
    onehot = (dest[:, None] == jnp.arange(span_count, dtype=jnp.int32)[None, :]).astype(jnp.int32)
    slots = jnp.sum((jnp.cumsum(onehot, axis=0) - 1) * onehot, axis=1)
    position = dest * slot_count + slots
    out_width = targets.shape[1]
    payload = jnp.concatenate([rows, targets], axis=1)
    width = payload.shape[1]
    empty = jnp.concatenate(
        [jnp.zeros((1, FEAT), jnp.bfloat16), jnp.full((1, out_width), EMPTY_MARK, jnp.bfloat16)], axis=1
    )
    buffer = jnp.broadcast_to(empty, (span_count * slot_count, width)).at[position].set(payload)
    got = lax.all_to_all(
        buffer.reshape(span_count, slot_count, width), "span", split_axis=0, concat_axis=0, tiled=True
    ).reshape(span_count * slot_count, width)
    inputs = got[:, :FEAT]
    wanted_raw = got[:, FEAT : FEAT + out_width].astype(jnp.float32)
    filled = wanted_raw[:, :1] < EMPTY_MARK / 2
    wanted = jnp.where(filled, wanted_raw, 0.0)
    flags = filled[:, 0].astype(jnp.float32)
    row_scale = flags / jnp.maximum(jnp.sum(flags), 1.0)
    layer_one = weight_in[0]
    layer_two = weight_two[0]
    layer_three = weight_three[0]
    layer_four = weight_four[0]
    layer_last = weight_out[0]
    weights = (layer_one, layer_two, layer_three, layer_four, layer_last)
    output, acts, pres = forward(inputs, weights)
    error = (row_scale[:, None] * (output - wanted)).astype(jnp.bfloat16)
    grad_last = weight_grad(acts[4], error)
    error = backward_layer(error, layer_last, pres[3])
    grad_fourth = weight_grad(acts[3], error)
    error = backward_layer(error, layer_four, pres[2])
    grad_third = weight_grad(acts[2], error)
    error = backward_layer(error, layer_three, pres[1])
    grad_second = weight_grad(acts[1], error)
    error = backward_layer(error, layer_two, pres[0])
    grad_first = weight_grad(acts[0], error)
    grads = (grad_first, grad_second, grad_third, grad_fourth, grad_last)
    summed = wall_sum(grads)
    return (new_field,) + tuple(g[None] for g in summed)


def wall_sum(grads):
    size = lax.axis_size("wall")
    groups = wall_groups(size)
    if groups is None:
        return lax.psum(grads, "wall")
    lanes = 128
    flat = jnp.concatenate([g.reshape(-1, lanes) for g in grads], axis=0)
    me = lax.axis_index("wall")
    scatter_groups = [(off, count) for off, count in groups if count > 2]
    exchange_groups = [(off, count) for off, count in groups if count <= 2]
    for off, count in scatter_groups:
        coord = (me >> off) & (count - 1)
        parts = flat.reshape(count, flat.shape[0] // count, lanes)
        total = lax.dynamic_index_in_dim(parts, coord, 0, keepdims=False)
        for shift in range(1, count):
            send = lax.dynamic_index_in_dim(parts, (coord + shift) % count, 0, keepdims=False)
            total = total + lax.ppermute(send, "wall", group_pairs(size, off, count, shift))
        flat = total
    for off, count in exchange_groups:
        flat = flat + lax.ppermute(flat, "wall", group_pairs(size, off, count, 1))
    for off, count in reversed(scatter_groups):
        coord = (me >> off) & (count - 1)
        sent = flat.astype(LINK_DTYPE)
        got = [sent] + [
            lax.ppermute(sent, "wall", group_pairs(size, off, count, shift)) for shift in range(1, count)
        ]
        stacked = jnp.stack(got)
        flat = jnp.concatenate(
            [
                lax.dynamic_index_in_dim(stacked, (coord - part) % count, 0, keepdims=False)
                for part in range(count)
            ],
            axis=0,
        )
    flat = flat.astype(jnp.float32)
    out = []
    at = 0
    for g in grads:
        rows_of = g.size // lanes
        out.append(flat[at : at + rows_of].reshape(g.shape))
        at += rows_of
    return tuple(out)


def wall_groups(size):
    if size != 32:
        return None
    return [(0, 4), (2, 4), (4, 2)]


def group_pairs(size, off, count, shift):
    pairs = []
    for i in range(size):
        coord = (i >> off) & (count - 1)
        dest = i - (coord << off) + (((coord + shift) % count) << off)
        pairs.append((i, dest))
    return pairs


def solution(mesh):
    in_specs = (
        P(None, None, None, "span", "wall", None),
        P(None, None, None, None, "span", "wall", None),
        P(("span", "wall")),
        P(("span", "wall"), None),
        P(("span", "wall"), None),
        P("span", None, None),
        P("span", None, None),
        P("span", None, None),
        P("span", None, None),
        P("span", None, None),
    )
    out_specs = (
        P(None, None, None, "span", "wall", None),
        P("span", None, None),
        P("span", None, None),
        P("span", None, None),
        P("span", None, None),
        P("span", None, None),
    )
    return jax.shard_map(local, mesh=mesh, in_specs=in_specs, out_specs=out_specs, check_vma=False)
```
